512 devices in a mesh: lon: 32 (over z, core), lat: 16 (over x, y).
Axes of the slice: x: 4, y: 4, z: 16, core: 2. Of those that a mesh axis runs over, the one named last changes fastest.
Arguments:
- iterate: float32 [127, 16, 4096], P(None, 'lat', 'lon'), may hold values from -200 to 200
- residual: float32 [127, 16, 4096], P(None, 'lat', 'lon'), may hold values from -200 to 200
- direction: float32 [127, 16, 4096], P(None, 'lat', 'lon'), may hold values from -200 to 200
- obs_weight: float32 [127, 16, 4096], P(None, 'lat', 'lon'), may hold values from 0.5 to 5
- vertical: float32 [127, 127], replicated, may hold values from -0.2 to 1.2
- lon_taps: float32 [32, 101], replicated, may hold values from 0 to 1
- lat_taps: float32 [32, 101], replicated, may hold values from 0 to 1
- band_sizes: int32 [32], replicated, may hold values from 1 to 12, 127 in all
Outputs:
- iterate_next: float32 [127, 16, 4096], P(None, 'lat', 'lon')
- residual_next: float32 [127, 16, 4096], P(None, 'lat', 'lon')
- direction_next: float32 [127, 16, 4096], P(None, 'lat', 'lon')
The draws below stay inside these ranges and needn't reach their ends.
Inputs may be any that keep to these rules, and one draw needn't show every extreme that they name: `band_sizes`: the bands sum to 127 levels and the largest holds exactly 12 levels.
All inputs are finite; a program needn't handle non-finite values.
Results may differ from the reference program's by a relative error of at most 0.000071.
Values sent between devices are 32-bit elements; how exact they have to be, the bound alone decides.
No kernel may reach another device: no remote copies, remote signals or barrier semaphores. Data moves between devices by JAX's collectives and lax.ppermute only.
A program may use at most 64 MiB of HBM per device.

```python
import math
import jax
import jax.numpy as jnp
import numpy as np
from jax import lax

LEV = 127
TAPS = 101
HALF = 50
GROUPS = 32
MOST = 12
NLAT = 16
NLON = 4096


def rough_field(key, salt):
    subkeys = jax.random.split(jax.random.fold_in(key, salt), 4)
    noise_part = jnp.clip(jax.random.normal(subkeys[0], (LEV, NLAT, NLON), jnp.float32), -6.0, 6.0)
    rise_rate = 0.5
    level_scale = jnp.exp(jax.random.uniform(subkeys[1], (LEV,), jnp.float32, math.log(0.3), math.log(3.0)))
    row_scale = jnp.exp(jax.random.uniform(subkeys[2], (NLAT,), jnp.float32, math.log(0.3), math.log(3.0)))
    column_scale = jnp.exp(jax.random.uniform(subkeys[3], (NLON,), jnp.float32, math.log(0.3), math.log(3.0)))
    row_trend = 3.0 ** (rise_rate * jnp.arange(NLAT, dtype=jnp.float32) / NLAT)
    column_trend = 3.0 ** (rise_rate * jnp.arange(NLON, dtype=jnp.float32) / NLON)
    rows = row_scale * row_trend
    columns = column_scale * column_trend
    return noise_part * level_scale[:, None, None] * rows[None, :, None] * columns[None, None, :] / 3.0


def smooth_kernel(key, salt):
    subkeys = jax.random.split(jax.random.fold_in(key, salt), 2)
    scales = jnp.exp(jax.random.uniform(subkeys[0], (GROUPS,), jnp.float32, math.log(2.0), math.log(40.0)))
    offsets = jnp.arange(TAPS, dtype=jnp.float32) - (TAPS - 1) // 2
    profile = jnp.exp(-offsets[None, :] ** 2 / (2.0 * scales[:, None] ** 2))
    profile = profile * jax.random.uniform(subkeys[1], (GROUPS, TAPS), jnp.float32, 0.5, 1.5)
    return profile / jnp.sqrt(jnp.sum(profile * profile, axis=1, keepdims=True))


def draw_iterate(key, part):
    return rough_field(key, 11)


def draw_residual(key, part):
    return rough_field(key, 12)


def draw_direction(key, part):
    return rough_field(key, 13)


def draw_vertical(key, part):
    subkey = jax.random.fold_in(key, 21)
    spread = jnp.clip(jax.random.normal(subkey, (LEV, LEV), jnp.float32), -4.0, 4.0)
    return jnp.eye(LEV, dtype=jnp.float32) + 0.5 * spread / math.sqrt(LEV)


def draw_lon_taps(key, part):
    return smooth_kernel(key, 31)


def draw_lat_taps(key, part):
    return smooth_kernel(key, 32)


def level_of(own_key, extent, pieces, smallest, high):
    factor_of, own = 1.0, jax.random.fold_in(own_key, 6)
    for position, blocks in pieces:
        draws = jnp.exp(jax.random.uniform(jax.random.fold_in(own, position), (blocks,), jnp.float32, smallest / len(pieces), high / len(pieces)))
        factor_of = factor_of * jnp.repeat(draws, extent[position] // blocks).reshape([-1 if axis == position else 1 for axis in range(len(extent))])
    return factor_of


def length_profile(amount, total, most, slope):
    loads = [(1 << 20) // math.isqrt(standing ** slope) + 1 for standing in range(2, amount + 1)]
    spare, holding = total - most - (amount - 1), [1] * (amount - 1)
    while spare > 0:
        candidates = [i for i in range(amount - 1) if holding[i] < most]
        pool, remaining = sum([loads[i] for i in candidates]), spare
        for i in candidates:
            addition = min(most - holding[i], max(1, remaining * loads[i] // pool), spare)
            holding[i] = holding[i] + addition
            spare = spare - addition
    return np.array([most] + holding)


def uneven(stream_key, count, total, most, lean):
    if count == 2:
        one = jax.random.randint(stream_key, (), max(1, total - most), min(most, total - 1) + 1)
        return jnp.stack([one, total - one])
    tallies = jnp.asarray(length_profile(count, total, most, lean), jnp.int32)
    twos = (count - 1) // 2
    giver, sink = tallies[1:1 + 2 * twos:2], tallies[2:2 + 2 * twos:2]
    slack = jnp.minimum(giver - 1, most - sink)
    moved = jax.random.randint(jax.random.fold_in(stream_key, 1), (twos,), 0, 1 << 20) % (slack + 1)
    tallies = tallies.at[1:1 + 2 * twos:2].set(giver - moved).at[2:2 + 2 * twos:2].set(sink + moved)
    return tallies[jax.random.permutation(jax.random.fold_in(stream_key, 2), count)]


def setup_inputs(seed: int = 0) -> dict:
    arg_keys = jax.random.split(jax.random.key(seed), 9)
    iterate = draw_iterate(jax.random.fold_in(arg_keys[8], 71), 0)
    residual = draw_residual(jax.random.fold_in(arg_keys[8], 71), 0)
    direction = draw_direction(jax.random.fold_in(arg_keys[8], 71), 0)
    obs_weight = jnp.clip(jnp.exp(math.log(5.0) - 2.3025851 * jax.random.uniform(arg_keys[3], (LEV, NLAT, NLON), jnp.float32) ** level_of(arg_keys[3], (LEV, NLAT, NLON), ((1, 16), (2, 32)), -0.2, 0.2)), 0.5, 5.0)
    vertical = draw_vertical(jax.random.fold_in(arg_keys[8], 71), 0)
    lon_taps = draw_lon_taps(jax.random.fold_in(arg_keys[8], 71), 0)
    lat_taps = draw_lat_taps(jax.random.fold_in(arg_keys[8], 71), 0)
    band_sizes = uneven(arg_keys[7], GROUPS, LEV, MOST, 2).astype(jnp.int32)
    return {"iterate": iterate, "residual": residual, "direction": direction, "obs_weight": obs_weight, "vertical": vertical, "lon_taps": lon_taps, "lat_taps": lat_taps, "band_sizes": band_sizes}


HIGHEST = lax.Precision.HIGHEST


def band_matrices(kernel, width_in, width_out, anchor):
    offsets = jnp.arange(width_in, dtype=jnp.int32)[:, None] - anchor - jnp.arange(width_out, dtype=jnp.int32)[None, :] + HALF
    inside = (offsets >= 0) & (offsets < TAPS)
    picked = kernel[:, jnp.clip(offsets, 0, TAPS - 1)]
    return jnp.where(inside[None], picked, jnp.zeros_like(picked))


def level_groups(band_sizes):
    bounds = jnp.cumsum(band_sizes).astype(jnp.int32)
    levels = jnp.arange(LEV, dtype=jnp.int32)
    return jnp.sum((levels[:, None] >= bounds[None, :]).astype(jnp.int32), axis=1).astype(jnp.int32)


def along_lon(grid_field, kernel):
    block_count = NLON // 128

    def single(level_pair):
        plane, level_kernel = level_pair
        blocks = plane.reshape(NLAT, block_count, 128)
        window = jnp.concatenate([jnp.roll(blocks, 1, axis=1), blocks, jnp.roll(blocks, -1, axis=1)], axis=2)
        matrix = band_matrices(level_kernel[None], 384, 128, 128)[0]
        return jnp.einsum("anc,co->ano", window, matrix, precision=HIGHEST).reshape(NLAT, NLON)

    return lax.map(single, (grid_field, kernel))


def along_lat(grid_field, kernel):
    def single(level_pair):
        plane, level_kernel = level_pair
        matrix = band_matrices(level_kernel[None], NLAT, NLAT, 0)[0]
        return jnp.einsum("ca,cx->ax", matrix, plane, precision=HIGHEST)

    return lax.map(single, (grid_field, kernel))


def vertical_mix(matrix, grid_field):
    return jnp.dot(matrix, grid_field.reshape(LEV, -1), precision=HIGHEST).reshape(grid_field.shape)


def reference(iterate, residual, direction, obs_weight, vertical, lon_taps, lat_taps, band_sizes):
    groups = level_groups(band_sizes)
    lon_rows = lon_taps[groups]
    lat_rows = lat_taps[groups]
    lon_part = along_lon(direction, lon_rows)
    lat_part = along_lat(lon_part, lat_rows)
    lifted = vertical_mix(vertical, lat_part)
    weighted = obs_weight * lifted
    back_vert = vertical_mix(vertical.T, weighted)
    back_lat = along_lat(back_vert, lat_rows[:, ::-1])
    image = direction + along_lon(back_lat, lon_rows[:, ::-1])
    norm_old = jnp.sum(residual * residual)
    curvature = jnp.sum(direction * image)
    alpha = norm_old / curvature
    iterate_next = iterate + alpha * direction
    residual_next = residual - alpha * image
    norm_new = jnp.sum(residual_next * residual_next)
    direction_next = residual_next + (norm_new / norm_old) * direction
    return iterate_next, residual_next, direction_next
```

```python
import jax
import jax.numpy as jnp
from jax import lax
from jax.sharding import PartitionSpec as P

LEV = 127
TAPS = 101
HALF = 50
GROUPS = 32


HIGHEST = lax.Precision.HIGHEST


def with_halo(cells, sides, width):
    for axis, dim in sides:
        count = lax.axis_size(axis)
        head = lax.slice_in_dim(cells, 0, width, axis=dim)
        tail = lax.slice_in_dim(cells, cells.shape[dim] - width, cells.shape[dim], axis=dim)
        cells = jnp.concatenate(
            [
                lax.ppermute(tail, axis, [(i, (i + 1) % count) for i in range(count)]),
                cells,
                lax.ppermute(head, axis, [((i + 1) % count, i) for i in range(count)]),
            ],
            axis=dim,
        )
    return cells


def band_matrices(kernel, width_in, width_out):
    offsets = (
        jnp.arange(width_in, dtype=jnp.int32)[:, None]
        - jnp.arange(width_out, dtype=jnp.int32)[None, :]
        + HALF
    )
    inside = (offsets >= 0) & (offsets < TAPS)
    picked = kernel[:, jnp.clip(offsets, 0, TAPS - 1)]
    return jnp.where(inside[None], picked, jnp.zeros_like(picked))


def group_rows(group_ids, kernel):
    onehot = (group_ids[:, None] == jnp.arange(GROUPS, dtype=jnp.int32)[None, :]).astype(
        jnp.float32
    )
    return jnp.dot(onehot, kernel, precision=HIGHEST)


def slot_plan(groups, devices_count):
    levels = jnp.arange(LEV, dtype=jnp.int32)
    capacity = (LEV + devices_count - 1) // devices_count
    slot_ids = jnp.arange(devices_count * capacity, dtype=jnp.int32)
    matched = levels[None, :] == slot_ids[:, None]
    occupied = jnp.any(matched, axis=1)
    sources = jnp.sum(jnp.where(matched, levels[None, :], 0), axis=1)
    sources = jnp.where(occupied, sources, LEV)
    slot_groups = jnp.sum(jnp.where(matched, groups[None, :], 0), axis=1)
    return (capacity, levels, sources, slot_groups)


def into_slots(grid_field, sources):
    padded = jnp.concatenate(
        [grid_field, jnp.zeros((1,) + grid_field.shape[1:], grid_field.dtype)], axis=0
    )
    return jnp.take(padded, sources, axis=0)


def lon_pass(grid_field, kernel_groups, groups, adjoint):
    kernel = kernel_groups[:, ::-1] if adjoint else kernel_groups
    lon_width = grid_field.shape[2]
    kernels = group_rows(groups, kernel)
    extended = with_halo(grid_field, (("lon", 2),), HALF)
    windows = jnp.stack(
        [extended[:, :, shift_tap : shift_tap + lon_width] for shift_tap in range(TAPS)], axis=2
    )
    return jnp.einsum("lakb,lk->lab", windows, kernels, precision=HIGHEST)


def lat_pass(grid_field, kernel_groups, groups, adjoint):
    kernel = kernel_groups[:, ::-1] if adjoint else kernel_groups
    devices_count = lax.axis_size("lat")
    capacity, position, sources, slot_groups = slot_plan(groups, devices_count)
    slotted = into_slots(grid_field, sources)
    own_groups = lax.dynamic_slice_in_dim(slot_groups, lax.axis_index("lat") * capacity, capacity)
    lat_width = grid_field.shape[1] * devices_count
    matrices = band_matrices(group_rows(own_groups, kernel), lat_width, lat_width)
    filtered = jnp.einsum(
        "sco,scx->sox",
        matrices,
        lax.all_to_all(slotted, "lat", split_axis=0, concat_axis=1, tiled=True),
        precision=HIGHEST,
    )
    returned = lax.all_to_all(filtered, "lat", split_axis=1, concat_axis=0, tiled=True)
    return jnp.take(returned, position, axis=0)


def vertical_mix(matrix, grid_field):
    return jnp.dot(matrix, grid_field.reshape(LEV, -1), precision=HIGHEST).reshape(grid_field.shape)


def total(vals):
    v = jnp.stack(vals)
    for axis in ("lat", "lon"):
        n = lax.axis_size(axis)
        g = lax.all_to_all(jnp.broadcast_to(v[None], (n,) + v.shape), axis, 0, 0, tiled=True)
        v = jnp.sum(g, axis=0)
    return tuple(v[i] for i in range(len(vals)))


def local(iterate, residual, direction, obs_weight, vertical, lon_taps, lat_taps, band_sizes):
    bounds = jnp.cumsum(band_sizes)
    levels = jnp.arange(LEV, dtype=jnp.int32)
    groups = jnp.sum((levels[:, None] >= bounds[None, :]).astype(jnp.int32), axis=1)
    lon_part = lon_pass(direction, lon_taps, groups, False)
    lat_part = lat_pass(lon_part, lat_taps, groups, False)
    lifted = vertical_mix(vertical, lat_part)
    weighted = obs_weight * lifted
    back_vert = vertical_mix(vertical.T, weighted)
    back_lat = lat_pass(back_vert, lat_taps, groups, True)
    applied = direction + lon_pass(back_lat, lon_taps, groups, True)
    norm_old, curvature = total((jnp.sum(residual * residual), jnp.sum(direction * applied)))
    step_length = norm_old / curvature
    residual_next = residual - step_length * applied
    (norm_new,) = total((jnp.sum(residual_next * residual_next),))
    iterate_next = iterate + step_length * direction
    direction_next = residual_next + norm_new / norm_old * direction
    return (iterate_next, residual_next, direction_next)


def solution(mesh):
    placed = (
        P(None, "lat", "lon"),
        P(None, "lat", "lon"),
        P(None, "lat", "lon"),
        P(None, "lat", "lon"),
        P(),
        P(),
        P(),
        P(),
    )
    return jax.shard_map(
        local,
        mesh=mesh,
        in_specs=placed,
        out_specs=(P(None, "lat", "lon"), P(None, "lat", "lon"), P(None, "lat", "lon")),
        check_vma=False,
    )
```

```python
import jax
import jax.numpy as jnp
from jax import lax
from jax.sharding import PartitionSpec as P

LEV = 127
TAPS = 101
HALF = 50
GROUPS = 32


HIGHEST = lax.Precision.HIGHEST


def with_halo(cells, sides, width):
    for axis, dim in sides:
        count = lax.axis_size(axis)
        head = lax.slice_in_dim(cells, 0, width, axis=dim)
        tail = lax.slice_in_dim(cells, cells.shape[dim] - width, cells.shape[dim], axis=dim)
        cells = jnp.concatenate(
            [
                lax.ppermute(tail, axis, [(i, (i + 1) % count) for i in range(count)]),
                cells,
                lax.ppermute(head, axis, [((i + 1) % count, i) for i in range(count)]),
            ],
            axis=dim,
        )
    return cells


def band_matrices(kernel, width_in, width_out):
    offsets = (
        jnp.arange(width_in, dtype=jnp.int32)[:, None]
        - jnp.arange(width_out, dtype=jnp.int32)[None, :]
        + HALF
    )
    inside = (offsets >= 0) & (offsets < TAPS)
    picked = kernel[:, jnp.clip(offsets, 0, TAPS - 1)]
    return jnp.where(inside[None], picked, jnp.zeros_like(picked))


def group_rows(group_ids, kernel):
    onehot = (group_ids[:, None] == jnp.arange(GROUPS, dtype=jnp.int32)[None, :]).astype(
        jnp.float32
    )
    return jnp.dot(onehot, kernel, precision=HIGHEST)


def slot_plan(groups, devices_count):
    levels = jnp.arange(LEV, dtype=jnp.int32)
    capacity = (LEV + devices_count - 1) // devices_count
    slot_ids = jnp.arange(devices_count * capacity, dtype=jnp.int32)
    matched = levels[None, :] == slot_ids[:, None]
    occupied = jnp.any(matched, axis=1)
    sources = jnp.sum(jnp.where(matched, levels[None, :], 0), axis=1)
    sources = jnp.where(occupied, sources, LEV)
    slot_groups = jnp.sum(jnp.where(matched, groups[None, :], 0), axis=1)
    return (capacity, levels, sources, slot_groups)


def into_slots(grid_field, sources):
    padded = jnp.concatenate(
        [grid_field, jnp.zeros((1,) + grid_field.shape[1:], grid_field.dtype)], axis=0
    )
    return jnp.take(padded, sources, axis=0)


def lon_pass(grid_field, kernel_groups, groups, adjoint):
    kernel = kernel_groups[:, ::-1] if adjoint else kernel_groups
    lon_width = grid_field.shape[2]
    kernels = group_rows(groups, kernel)
    extended = with_halo(grid_field, (("lon", 2),), HALF)
    total_sum = kernels[:, None, 0:1] * extended[:, :, 0:lon_width]
    for shift_tap in range(1, TAPS):
        total_sum = total_sum + kernels[:, None, shift_tap : shift_tap + 1] * extended[
            :, :, shift_tap : shift_tap + lon_width
        ]
    return total_sum


def lat_pass(grid_field, kernel_groups, groups, adjoint):
    kernel = kernel_groups[:, ::-1] if adjoint else kernel_groups
    rows = grid_field.shape[1]
    full = lax.all_gather(grid_field, "lat", axis=1, tiled=True)
    lat_width = full.shape[1]
    own = lax.axis_index("lat") * rows + jnp.arange(rows, dtype=jnp.int32)
    offsets = jnp.arange(lat_width, dtype=jnp.int32)[:, None] - own[None, :] + HALF
    inside = (offsets >= 0) & (offsets < TAPS)
    picked = group_rows(groups, kernel)[:, jnp.clip(offsets, 0, TAPS - 1)]
    matrices = jnp.where(inside[None], picked, jnp.zeros_like(picked))
    return jnp.sum(matrices[:, :, :, None] * full[:, :, None, :], axis=1)


def vertical_mix(matrix, grid_field):
    return jnp.dot(matrix, grid_field.reshape(LEV, -1), precision=HIGHEST).reshape(grid_field.shape)


def total(vals):
    v = jnp.stack(vals)
    for axis in ("lat", "lon"):
        n = lax.axis_size(axis)
        g = lax.all_to_all(jnp.broadcast_to(v[None], (n,) + v.shape), axis, 0, 0, tiled=True)
        v = jnp.sum(g, axis=0)
    return tuple(v[i] for i in range(len(vals)))


def local(iterate, residual, direction, obs_weight, vertical, lon_taps, lat_taps, band_sizes):
    bounds = jnp.cumsum(band_sizes)
    levels = jnp.arange(LEV, dtype=jnp.int32)
    groups = jnp.sum((levels[:, None] >= bounds[None, :]).astype(jnp.int32), axis=1)
    lon_part = lon_pass(direction, lon_taps, groups, False)
    lat_part = lat_pass(lon_part, lat_taps, groups, False)
    lifted = vertical_mix(vertical, lat_part)
    weighted = obs_weight * lifted
    back_vert = vertical_mix(vertical.T, weighted)
    back_lat = lat_pass(back_vert, lat_taps, groups, True)
    applied = direction + lon_pass(back_lat, lon_taps, groups, True)
    norm_old, curvature = total((jnp.sum(residual * residual), jnp.sum(direction * applied)))
    step_length = norm_old / curvature
    residual_next = residual - step_length * applied
    (norm_new,) = total((jnp.sum(residual_next * residual_next),))
    iterate_next = iterate + step_length * direction
    direction_next = residual_next + norm_new / norm_old * direction
    return (iterate_next, residual_next, direction_next)


def solution(mesh):
    placed = (
        P(None, "lat", "lon"),
        P(None, "lat", "lon"),
        P(None, "lat", "lon"),
        P(None, "lat", "lon"),
        P(),
        P(),
        P(),
        P(),
    )
    return jax.shard_map(
        local,
        mesh=mesh,
        in_specs=placed,
        out_specs=(P(None, "lat", "lon"), P(None, "lat", "lon"), P(None, "lat", "lon")),
        check_vma=False,
    )
```

```python
import jax
import jax.numpy as jnp
from jax import lax
from jax.sharding import PartitionSpec as P

LEV = 127
TAPS = 101
HALF = 50
GROUPS = 32


HIGHEST = lax.Precision.HIGHEST


def with_halo(cells, sides, width):
    for axis, dim in sides:
        count = lax.axis_size(axis)
        head = lax.slice_in_dim(cells, 0, width, axis=dim)
        tail = lax.slice_in_dim(cells, cells.shape[dim] - width, cells.shape[dim], axis=dim)
        cells = jnp.concatenate(
            [
                lax.ppermute(tail, axis, [(i, (i + 1) % count) for i in range(count)]),
                cells,
                lax.ppermute(head, axis, [((i + 1) % count, i) for i in range(count)]),
            ],
            axis=dim,
        )
    return cells


def band_matrices(kernel, width_in, width_out):
    offsets = (
        jnp.arange(width_in, dtype=jnp.int32)[:, None]
        - jnp.arange(width_out, dtype=jnp.int32)[None, :]
        + HALF
    )
    inside = (offsets >= 0) & (offsets < TAPS)
    picked = kernel[:, jnp.clip(offsets, 0, TAPS - 1)]
    return jnp.where(inside[None], picked, jnp.zeros_like(picked))


def group_rows(group_ids, kernel):
    onehot = (group_ids[:, None] == jnp.arange(GROUPS, dtype=jnp.int32)[None, :]).astype(
        jnp.float32
    )
    return jnp.dot(onehot, kernel, precision=HIGHEST)


def slot_plan(groups, devices_count):
    levels = jnp.arange(LEV, dtype=jnp.int32)
    capacity = (LEV + devices_count - 1) // devices_count
    slot_ids = jnp.arange(devices_count * capacity, dtype=jnp.int32)
    matched = levels[None, :] == slot_ids[:, None]
    occupied = jnp.any(matched, axis=1)
    sources = jnp.sum(jnp.where(matched, levels[None, :], 0), axis=1)
    sources = jnp.where(occupied, sources, LEV)
    slot_groups = jnp.sum(jnp.where(matched, groups[None, :], 0), axis=1)
    return (capacity, levels, sources, slot_groups)


def into_slots(grid_field, sources):
    padded = jnp.concatenate(
        [grid_field, jnp.zeros((1,) + grid_field.shape[1:], grid_field.dtype)], axis=0
    )
    return jnp.take(padded, sources, axis=0)


def lon_pass(grid_field, kernel_groups, groups, adjoint):
    kernel = kernel_groups[:, ::-1] if adjoint else kernel_groups
    lon_width = grid_field.shape[2]
    kernels = group_rows(groups, kernel)
    extended = with_halo(grid_field, (("lon", 2),), HALF)
    total_sum = kernels[:, None, 0:1] * extended[:, :, 0:lon_width]
    for shift_tap in range(1, TAPS):
        total_sum = total_sum + kernels[:, None, shift_tap : shift_tap + 1] * extended[
            :, :, shift_tap : shift_tap + lon_width
        ]
    return total_sum


def lat_pass(grid_field, kernel_groups, groups, adjoint):
    kernel = kernel_groups[:, ::-1] if adjoint else kernel_groups
    rows = grid_field.shape[1]
    full = lax.all_gather(grid_field, "lat", axis=1, tiled=True)
    lat_width = full.shape[1]
    own = lax.axis_index("lat") * rows + jnp.arange(rows, dtype=jnp.int32)
    offsets = jnp.arange(lat_width, dtype=jnp.int32)[:, None] - own[None, :] + HALF
    inside = (offsets >= 0) & (offsets < TAPS)
    picked = group_rows(groups, kernel)[:, jnp.clip(offsets, 0, TAPS - 1)]
    matrices = jnp.where(inside[None], picked, jnp.zeros_like(picked))
    return jnp.sum(matrices[:, :, :, None] * full[:, :, None, :], axis=1)


def vertical_mix(matrix, grid_field):
    return jnp.dot(matrix, grid_field.reshape(LEV, -1), precision=HIGHEST).reshape(grid_field.shape)


def total(vals):
    v = jnp.stack(vals)
    for axis in ("lat", "lon"):
        n = lax.axis_size(axis)
        g = lax.all_to_all(jnp.broadcast_to(v[None], (n,) + v.shape), axis, 0, 0, tiled=True)
        v = jnp.sum(g, axis=0)
    return tuple(v[i] for i in range(len(vals)))


def local(iterate, residual, direction, obs_weight, vertical, lon_taps, lat_taps, band_sizes):
    bounds = jnp.cumsum(band_sizes)
    levels = jnp.arange(LEV, dtype=jnp.int32)
    groups = jnp.sum((levels[:, None] >= bounds[None, :]).astype(jnp.int32), axis=1)
    lon_part = lon_pass(direction, lon_taps, groups, False)
    lat_part = lat_pass(lon_part, lat_taps, groups, False)
    lifted = vertical_mix(vertical, lat_part)
    weighted = obs_weight * lifted
    norm_old, curvature = total(
        (jnp.sum(residual * residual), jnp.sum(direction * direction) + jnp.sum(weighted * lifted))
    )
    back_vert = vertical_mix(vertical.T, weighted)
    back_lat = lat_pass(back_vert, lat_taps, groups, True)
    applied = lax.optimization_barrier(direction + lon_pass(back_lat, lon_taps, groups, True))
    step_length = norm_old / curvature
    residual_next = residual - step_length * applied
    (norm_new,) = total((jnp.sum(residual_next * residual_next),))
    iterate_next = iterate + step_length * direction
    direction_next = residual_next + norm_new / norm_old * direction
    return (iterate_next, residual_next, direction_next)


def solution(mesh):
    placed = (
        P(None, "lat", "lon"),
        P(None, "lat", "lon"),
        P(None, "lat", "lon"),
        P(None, "lat", "lon"),
        P(),
        P(),
        P(),
        P(),
    )
    return jax.shard_map(
        local,
        mesh=mesh,
        in_specs=placed,
        out_specs=(P(None, "lat", "lon"), P(None, "lat", "lon"), P(None, "lat", "lon")),
        check_vma=False,
    )
```

```python
import jax
import jax.numpy as jnp
from jax import lax
from jax.experimental import pallas as pl
from jax.sharding import PartitionSpec as P

LEV = 127
TAPS = 101
HALF = 50
GROUPS = 32


HIGHEST = lax.Precision.HIGHEST


def with_halo(cells, sides, width):
    for axis, dim in sides:
        count = lax.axis_size(axis)
        head = lax.slice_in_dim(cells, 0, width, axis=dim)
        tail = lax.slice_in_dim(cells, cells.shape[dim] - width, cells.shape[dim], axis=dim)
        cells = jnp.concatenate(
            [
                lax.ppermute(tail, axis, [(i, (i + 1) % count) for i in range(count)]),
                cells,
                lax.ppermute(head, axis, [((i + 1) % count, i) for i in range(count)]),
            ],
            axis=dim,
        )
    return cells


def band_matrices(kernel, width_in, width_out):
    offsets = (
        jnp.arange(width_in, dtype=jnp.int32)[:, None]
        - jnp.arange(width_out, dtype=jnp.int32)[None, :]
        + HALF
    )
    inside = (offsets >= 0) & (offsets < TAPS)
    picked = kernel[:, jnp.clip(offsets, 0, TAPS - 1)]
    return jnp.where(inside[None], picked, jnp.zeros_like(picked))


def group_rows(group_ids, kernel):
    onehot = (group_ids[:, None] == jnp.arange(GROUPS, dtype=jnp.int32)[None, :]).astype(
        jnp.float32
    )
    return jnp.dot(onehot, kernel, precision=HIGHEST)


def slot_plan(groups, devices_count):
    levels = jnp.arange(LEV, dtype=jnp.int32)
    capacity = (LEV + devices_count - 1) // devices_count
    slot_ids = jnp.arange(devices_count * capacity, dtype=jnp.int32)
    matched = levels[None, :] == slot_ids[:, None]
    occupied = jnp.any(matched, axis=1)
    sources = jnp.sum(jnp.where(matched, levels[None, :], 0), axis=1)
    sources = jnp.where(occupied, sources, LEV)
    slot_groups = jnp.sum(jnp.where(matched, groups[None, :], 0), axis=1)
    return (capacity, levels, sources, slot_groups)


def into_slots(grid_field, sources):
    padded = jnp.concatenate(
        [grid_field, jnp.zeros((1,) + grid_field.shape[1:], grid_field.dtype)], axis=0
    )
    return jnp.take(padded, sources, axis=0)


def lon_kernel(taps_ref, extended_ref, out_ref):
    width = out_ref.shape[1]
    total_sum = taps_ref[:, 0:1] * extended_ref[:, 0:width]
    for shift_tap in range(1, TAPS):
        total_sum = total_sum + taps_ref[:, shift_tap : shift_tap + 1] * extended_ref[
            :, shift_tap : shift_tap + width
        ]
    out_ref[...] = total_sum


def lon_pass(grid_field, kernel_groups, groups, adjoint):
    kernel = kernel_groups[:, ::-1] if adjoint else kernel_groups
    levels, rows, lon_width = grid_field.shape
    kernels = jnp.repeat(group_rows(groups, kernel), rows, axis=0)
    extended = with_halo(grid_field, (("lon", 2),), HALF)
    filtered = pl.pallas_call(
        lon_kernel, out_shape=jax.ShapeDtypeStruct((levels * rows, lon_width), grid_field.dtype)
    )(kernels, extended.reshape(levels * rows, -1))
    return filtered.reshape(levels, rows, lon_width)


def to_columns(grid_field):
    return lax.all_to_all(grid_field, "lat", 2, 1, tiled=True)


def to_rows(grid_field):
    return lax.all_to_all(grid_field, "lat", 1, 2, tiled=True)


def lat_pass(grid_field, kernel_groups, groups, adjoint):
    kernel = kernel_groups[:, ::-1] if adjoint else kernel_groups
    lat_width = grid_field.shape[1]
    matrices = band_matrices(group_rows(groups, kernel), lat_width, lat_width)
    return jnp.sum(matrices[:, :, :, None] * grid_field[:, :, None, :], axis=1)


def vertical_mix(matrix, grid_field):
    return jnp.dot(matrix, grid_field.reshape(LEV, -1), precision=HIGHEST).reshape(grid_field.shape)


def total(vals, axes=("lat", "lon")):
    v = jnp.stack(vals)
    for axis in axes:
        n = lax.axis_size(axis)
        g = lax.all_to_all(jnp.broadcast_to(v[None], (n,) + v.shape), axis, 0, 0, tiled=True)
        v = jnp.sum(g, axis=0)
    return tuple(v[i] for i in range(len(vals)))


def local(iterate, residual, direction, obs_weight, vertical, lon_taps, lat_taps, band_sizes):
    bounds = jnp.cumsum(band_sizes)
    levels = jnp.arange(LEV, dtype=jnp.int32)
    groups = jnp.sum((levels[:, None] >= bounds[None, :]).astype(jnp.int32), axis=1)
    lon_part = lon_pass(direction, lon_taps, groups, False)
    both = to_columns(jnp.concatenate([lon_part, obs_weight], axis=0))
    lat_part = lat_pass(both[:LEV], lat_taps, groups, False)
    lifted = vertical_mix(vertical, lat_part)
    weighted = both[LEV:] * lifted
    partial = jnp.stack(
        [jnp.sum(residual * residual), jnp.sum(direction * direction) + jnp.sum(weighted * lifted)]
    )
    back_vert = vertical_mix(vertical.T, weighted)
    back_cols = lat_pass(back_vert, lat_taps, groups, True)
    chunk = back_cols.shape[2]
    extra = jnp.zeros((1,) + back_cols.shape[1:], back_cols.dtype).at[0, :, :2].set(partial)
    returned = to_rows(jnp.concatenate([back_cols, extra], axis=0))
    back_lat = returned[:LEV]
    lat_sums = jnp.sum(returned[LEV, 0].reshape(-1, chunk)[:, :2], axis=0)
    norm_old, curvature = total((lat_sums[0], lat_sums[1]), ("lon",))
    applied = lax.optimization_barrier(direction + lon_pass(back_lat, lon_taps, groups, True))
    step_length = norm_old / curvature
    residual_next = residual - step_length * applied
    (norm_new,) = total((jnp.sum(residual_next * residual_next),))
    iterate_next = iterate + step_length * direction
    direction_next = residual_next + norm_new / norm_old * direction
    return (iterate_next, residual_next, direction_next)


def solution(mesh):
    placed = (
        P(None, "lat", "lon"),
        P(None, "lat", "lon"),
        P(None, "lat", "lon"),
        P(None, "lat", "lon"),
        P(),
        P(),
        P(),
        P(),
    )
    return jax.shard_map(
        local,
        mesh=mesh,
        in_specs=placed,
        out_specs=(P(None, "lat", "lon"), P(None, "lat", "lon"), P(None, "lat", "lon")),
        check_vma=False,
    )
```

```python
import jax
import jax.numpy as jnp
from jax import lax
from jax.experimental import pallas as pl
from jax.sharding import PartitionSpec as P

LEV = 127
TAPS = 101
HALF = 50
GROUPS = 32


HIGHEST = lax.Precision.HIGHEST


def with_halo(cells, sides, width):
    for axis, dim in sides:
        count = lax.axis_size(axis)
        head = lax.slice_in_dim(cells, 0, width, axis=dim)
        tail = lax.slice_in_dim(cells, cells.shape[dim] - width, cells.shape[dim], axis=dim)
        cells = jnp.concatenate(
            [
                lax.ppermute(tail, axis, [(i, (i + 1) % count) for i in range(count)]),
                cells,
                lax.ppermute(head, axis, [((i + 1) % count, i) for i in range(count)]),
            ],
            axis=dim,
        )
    return cells


def band_matrices(kernel, width_in, width_out):
    offsets = (
        jnp.arange(width_in, dtype=jnp.int32)[:, None]
        - jnp.arange(width_out, dtype=jnp.int32)[None, :]
        + HALF
    )
    inside = (offsets >= 0) & (offsets < TAPS)
    picked = kernel[:, jnp.clip(offsets, 0, TAPS - 1)]
    return jnp.where(inside[None], picked, jnp.zeros_like(picked))


def group_rows(group_ids, kernel):
    onehot = (group_ids[:, None] == jnp.arange(GROUPS, dtype=jnp.int32)[None, :]).astype(
        jnp.float32
    )
    return jnp.dot(onehot, kernel, precision=HIGHEST)


def slot_plan(groups, devices_count):
    levels = jnp.arange(LEV, dtype=jnp.int32)
    capacity = (LEV + devices_count - 1) // devices_count
    slot_ids = jnp.arange(devices_count * capacity, dtype=jnp.int32)
    matched = levels[None, :] == slot_ids[:, None]
    occupied = jnp.any(matched, axis=1)
    sources = jnp.sum(jnp.where(matched, levels[None, :], 0), axis=1)
    sources = jnp.where(occupied, sources, LEV)
    slot_groups = jnp.sum(jnp.where(matched, groups[None, :], 0), axis=1)
    return (capacity, levels, sources, slot_groups)


def into_slots(grid_field, sources):
    padded = jnp.concatenate(
        [grid_field, jnp.zeros((1,) + grid_field.shape[1:], grid_field.dtype)], axis=0
    )
    return jnp.take(padded, sources, axis=0)


def lon_kernel(taps_ref, extended_ref, out_ref):
    width = out_ref.shape[0]
    total_sum = taps_ref[0:1, :] * extended_ref[0:width, :]
    for shift_tap in range(1, TAPS):
        total_sum = total_sum + taps_ref[shift_tap : shift_tap + 1, :] * extended_ref[
            shift_tap : shift_tap + width, :
        ]
    out_ref[...] = total_sum


def lon_pass(grid_field, kernel_groups, groups, adjoint):
    kernel = kernel_groups[:, ::-1] if adjoint else kernel_groups
    levels, rows, lon_width = grid_field.shape
    kernels = jnp.repeat(group_rows(groups, kernel), rows, axis=0)
    extended = with_halo(grid_field, (("lon", 2),), HALF)
    filtered = pl.pallas_call(
        lon_kernel, out_shape=jax.ShapeDtypeStruct((lon_width, levels * rows), grid_field.dtype)
    )(kernels.T, extended.reshape(levels * rows, -1).T)
    return filtered.T.reshape(levels, rows, lon_width)


def to_columns(grid_field):
    return lax.all_to_all(grid_field, "lat", 2, 1, tiled=True)


def to_rows(grid_field):
    return lax.all_to_all(grid_field, "lat", 1, 2, tiled=True)


def lat_pass(grid_field, kernel_groups, groups, adjoint):
    kernel = kernel_groups[:, ::-1] if adjoint else kernel_groups
    lat_width = grid_field.shape[1]
    matrices = band_matrices(group_rows(groups, kernel), lat_width, lat_width)
    return jnp.sum(matrices[:, :, :, None] * grid_field[:, :, None, :], axis=1)


def vertical_mix(matrix, grid_field):
    return jnp.dot(matrix, grid_field.reshape(LEV, -1), precision=HIGHEST).reshape(grid_field.shape)


def total(vals, axes=("lat", "lon")):
    v = jnp.stack(vals)
    for axis in axes:
        n = lax.axis_size(axis)
        g = lax.all_to_all(jnp.broadcast_to(v[None], (n,) + v.shape), axis, 0, 0, tiled=True)
        v = jnp.sum(g, axis=0)
    return tuple(v[i] for i in range(len(vals)))


def local(iterate, residual, direction, obs_weight, vertical, lon_taps, lat_taps, band_sizes):
    bounds = jnp.cumsum(band_sizes)
    levels = jnp.arange(LEV, dtype=jnp.int32)
    groups = jnp.sum((levels[:, None] >= bounds[None, :]).astype(jnp.int32), axis=1)
    lon_part = lon_pass(direction, lon_taps, groups, False)
    both = to_columns(jnp.concatenate([lon_part, obs_weight], axis=0))
    lat_part = lat_pass(both[:LEV], lat_taps, groups, False)
    lifted = vertical_mix(vertical, lat_part)
    weighted = both[LEV:] * lifted
    partial = jnp.stack(
        [jnp.sum(residual * residual), jnp.sum(direction * direction) + jnp.sum(weighted * lifted)]
    )
    back_vert = vertical_mix(vertical.T, weighted)
    back_cols = lat_pass(back_vert, lat_taps, groups, True)
    chunk = back_cols.shape[2]
    extra = jnp.zeros((1,) + back_cols.shape[1:], back_cols.dtype).at[0, :, :2].set(partial)
    returned = to_rows(jnp.concatenate([back_cols, extra], axis=0))
    back_lat = returned[:LEV]
    lat_sums = jnp.sum(returned[LEV, 0].reshape(-1, chunk)[:, :2], axis=0)
    norm_old, curvature = total((lat_sums[0], lat_sums[1]), ("lon",))
    applied = lax.optimization_barrier(direction + lon_pass(back_lat, lon_taps, groups, True))
    step_length = norm_old / curvature
    residual_next = residual - step_length * applied
    (norm_new,) = total((jnp.sum(residual_next * residual_next),))
    iterate_next = iterate + step_length * direction
    direction_next = residual_next + norm_new / norm_old * direction
    return (iterate_next, residual_next, direction_next)


def solution(mesh):
    placed = (
        P(None, "lat", "lon"),
        P(None, "lat", "lon"),
        P(None, "lat", "lon"),
        P(None, "lat", "lon"),
        P(),
        P(),
        P(),
        P(),
    )
    return jax.shard_map(
        local,
        mesh=mesh,
        in_specs=placed,
        out_specs=(P(None, "lat", "lon"), P(None, "lat", "lon"), P(None, "lat", "lon")),
        check_vma=False,
    )
```

```python
import jax
import jax.numpy as jnp
from jax import lax
from jax.experimental import pallas as pl
from jax.sharding import PartitionSpec as P

LEV = 127
TAPS = 101
HALF = 50
GROUPS = 32


HIGHEST = lax.Precision.HIGHEST


def with_halo(cells, sides, width):
    for axis, dim in sides:
        count = lax.axis_size(axis)
        head = lax.slice_in_dim(cells, 0, width, axis=dim)
        tail = lax.slice_in_dim(cells, cells.shape[dim] - width, cells.shape[dim], axis=dim)
        cells = jnp.concatenate(
            [
                lax.ppermute(tail, axis, [(i, (i + 1) % count) for i in range(count)]),
                cells,
                lax.ppermute(head, axis, [((i + 1) % count, i) for i in range(count)]),
            ],
            axis=dim,
        )
    return cells


def band_matrices(kernel, width_in, width_out):
    offsets = (
        jnp.arange(width_in, dtype=jnp.int32)[:, None]
        - jnp.arange(width_out, dtype=jnp.int32)[None, :]
        + HALF
    )
    inside = (offsets >= 0) & (offsets < TAPS)
    picked = kernel[:, jnp.clip(offsets, 0, TAPS - 1)]
    return jnp.where(inside[None], picked, jnp.zeros_like(picked))


def group_rows(group_ids, kernel):
    onehot = (group_ids[:, None] == jnp.arange(GROUPS, dtype=jnp.int32)[None, :]).astype(
        jnp.float32
    )
    return jnp.dot(onehot, kernel, precision=HIGHEST)


def slot_plan(groups, devices_count):
    levels = jnp.arange(LEV, dtype=jnp.int32)
    capacity = (LEV + devices_count - 1) // devices_count
    slot_ids = jnp.arange(devices_count * capacity, dtype=jnp.int32)
    matched = levels[None, :] == slot_ids[:, None]
    occupied = jnp.any(matched, axis=1)
    sources = jnp.sum(jnp.where(matched, levels[None, :], 0), axis=1)
    sources = jnp.where(occupied, sources, LEV)
    slot_groups = jnp.sum(jnp.where(matched, groups[None, :], 0), axis=1)
    return (capacity, levels, sources, slot_groups)


def into_slots(grid_field, sources):
    padded = jnp.concatenate(
        [grid_field, jnp.zeros((1,) + grid_field.shape[1:], grid_field.dtype)], axis=0
    )
    return jnp.take(padded, sources, axis=0)


def lon_kernel(taps_ref, extended_ref, out_ref):
    width = out_ref.shape[0]
    total_sum = taps_ref[0:1, :] * extended_ref[0:width, :]
    for shift_tap in range(1, TAPS):
        total_sum = total_sum + taps_ref[shift_tap : shift_tap + 1, :] * extended_ref[
            shift_tap : shift_tap + width, :
        ]
    out_ref[...] = total_sum


def lon_pass(grid_field, kernel_groups, groups, adjoint):
    kernel = kernel_groups[:, ::-1] if adjoint else kernel_groups
    levels, rows, lon_width = grid_field.shape
    kernels = jnp.repeat(group_rows(groups, kernel), rows, axis=0)
    extended = with_halo(grid_field, (("lon", 2),), HALF)
    filtered = pl.pallas_call(
        lon_kernel, out_shape=jax.ShapeDtypeStruct((lon_width, levels * rows), grid_field.dtype)
    )(kernels.T, extended.reshape(levels * rows, -1).T)
    return filtered.T.reshape(levels, rows, lon_width)


def to_columns(grid_field):
    return lax.all_to_all(grid_field, "lat", 2, 1, tiled=True)


def to_rows(grid_field):
    return lax.all_to_all(grid_field, "lat", 1, 2, tiled=True)


def lat_pass(grid_field, matrices, adjoint):
    if adjoint:
        return jnp.sum(matrices[:, :, :, None] * grid_field[:, None, :, :], axis=2)
    return jnp.sum(matrices[:, :, :, None] * grid_field[:, :, None, :], axis=1)


def vertical_mix(matrix, grid_field):
    return jnp.dot(matrix, grid_field.reshape(LEV, -1), precision=HIGHEST).reshape(grid_field.shape)


def total(vals, axes=("lat", "lon")):
    v = jnp.stack(vals)
    for axis in axes:
        n = lax.axis_size(axis)
        g = lax.all_to_all(jnp.broadcast_to(v[None], (n,) + v.shape), axis, 0, 0, tiled=True)
        v = jnp.sum(g, axis=0)
    return tuple(v[i] for i in range(len(vals)))


def local(iterate, residual, direction, obs_weight, vertical, lon_taps, lat_taps, band_sizes):
    bounds = jnp.cumsum(band_sizes)
    levels = jnp.arange(LEV, dtype=jnp.int32)
    groups = jnp.sum((levels[:, None] >= bounds[None, :]).astype(jnp.int32), axis=1)
    lon_part = lon_pass(direction, lon_taps, groups, False)
    both = to_columns(jnp.concatenate([lon_part, obs_weight], axis=0))
    lat_width = both.shape[1]
    matrices = band_matrices(group_rows(groups, lat_taps), lat_width, lat_width)
    lat_part = lat_pass(both[:LEV], matrices, False)
    lifted = vertical_mix(vertical, lat_part)
    weighted = both[LEV:] * lifted
    partial = jnp.stack(
        [jnp.sum(residual * residual), jnp.sum(direction * direction) + jnp.sum(weighted * lifted)]
    )
    back_vert = vertical_mix(vertical.T, weighted)
    back_cols = lat_pass(back_vert, matrices, True)
    chunk = back_cols.shape[2]
    extra = jnp.zeros((1,) + back_cols.shape[1:], back_cols.dtype).at[0, :, :2].set(partial)
    returned = to_rows(jnp.concatenate([back_cols, extra], axis=0))
    back_lat = returned[:LEV]
    lat_sums = jnp.sum(returned[LEV, 0].reshape(-1, chunk)[:, :2], axis=0)
    norm_old, curvature = total((lat_sums[0], lat_sums[1]), ("lon",))
    applied = lax.optimization_barrier(direction + lon_pass(back_lat, lon_taps, groups, True))
    step_length = norm_old / curvature
    residual_next = residual - step_length * applied
    (norm_new,) = total((jnp.sum(residual_next * residual_next),))
    iterate_next = iterate + step_length * direction
    direction_next = residual_next + norm_new / norm_old * direction
    return (iterate_next, residual_next, direction_next)


def solution(mesh):
    placed = (
        P(None, "lat", "lon"),
        P(None, "lat", "lon"),
        P(None, "lat", "lon"),
        P(None, "lat", "lon"),
        P(),
        P(),
        P(),
        P(),
    )
    return jax.shard_map(
        local,
        mesh=mesh,
        in_specs=placed,
        out_specs=(P(None, "lat", "lon"), P(None, "lat", "lon"), P(None, "lat", "lon")),
        check_vma=False,
    )
```

```python
import jax
import jax.numpy as jnp
from jax import lax
from jax.experimental import pallas as pl
from jax.sharding import PartitionSpec as P

LEV = 127
TAPS = 101
HALF = 50
GROUPS = 32


HIGHEST = lax.Precision.HIGHEST


def with_halo(cells, sides, width):
    for axis, dim in sides:
        count = lax.axis_size(axis)
        head = lax.slice_in_dim(cells, 0, width, axis=dim)
        tail = lax.slice_in_dim(cells, cells.shape[dim] - width, cells.shape[dim], axis=dim)
        cells = jnp.concatenate(
            [
                lax.ppermute(tail, axis, [(i, (i + 1) % count) for i in range(count)]),
                cells,
                lax.ppermute(head, axis, [((i + 1) % count, i) for i in range(count)]),
            ],
            axis=dim,
        )
    return cells


def band_matrices(kernel, width_in, width_out):
    offsets = (
        jnp.arange(width_in, dtype=jnp.int32)[:, None]
        - jnp.arange(width_out, dtype=jnp.int32)[None, :]
        + HALF
    )
    inside = (offsets >= 0) & (offsets < TAPS)
    picked = kernel[:, jnp.clip(offsets, 0, TAPS - 1)]
    return jnp.where(inside[None], picked, jnp.zeros_like(picked))


def group_rows(group_ids, kernel):
    onehot = (group_ids[:, None] == jnp.arange(GROUPS, dtype=jnp.int32)[None, :]).astype(
        jnp.float32
    )
    return jnp.dot(onehot, kernel, precision=HIGHEST)


def slot_plan(groups, devices_count):
    levels = jnp.arange(LEV, dtype=jnp.int32)
    capacity = (LEV + devices_count - 1) // devices_count
    slot_ids = jnp.arange(devices_count * capacity, dtype=jnp.int32)
    matched = levels[None, :] == slot_ids[:, None]
    occupied = jnp.any(matched, axis=1)
    sources = jnp.sum(jnp.where(matched, levels[None, :], 0), axis=1)
    sources = jnp.where(occupied, sources, LEV)
    slot_groups = jnp.sum(jnp.where(matched, groups[None, :], 0), axis=1)
    return (capacity, levels, sources, slot_groups)


def into_slots(grid_field, sources):
    padded = jnp.concatenate(
        [grid_field, jnp.zeros((1,) + grid_field.shape[1:], grid_field.dtype)], axis=0
    )
    return jnp.take(padded, sources, axis=0)


def lon_kernel(taps_ref, extended_ref, out_ref):
    width = out_ref.shape[0]
    total_sum = taps_ref[0:1, :] * extended_ref[0:width, :]
    for shift_tap in range(1, TAPS):
        total_sum = total_sum + taps_ref[shift_tap : shift_tap + 1, :] * extended_ref[
            shift_tap : shift_tap + width, :
        ]
    out_ref[...] = total_sum


def lon_pass(grid_field, kernel_groups, groups, adjoint):
    kernel = kernel_groups[:, ::-1] if adjoint else kernel_groups
    levels, rows, lon_width = grid_field.shape
    kernels = jnp.repeat(group_rows(groups, kernel), rows, axis=0)
    extended = with_halo(grid_field, (("lon", 2),), HALF)
    filtered = pl.pallas_call(
        lon_kernel, out_shape=jax.ShapeDtypeStruct((lon_width, levels * rows), grid_field.dtype)
    )(kernels.T, extended.reshape(levels * rows, -1).T)
    return filtered.T.reshape(levels, rows, lon_width)


def to_columns(grid_field):
    return lax.all_to_all(grid_field, "lat", 2, 1, tiled=True)


def to_rows(grid_field):
    return lax.all_to_all(grid_field, "lat", 1, 2, tiled=True)


def lat_pass(grid_field, matrices, adjoint):
    if adjoint:
        return jnp.sum(matrices[:, :, :, None] * grid_field[:, None, :, :], axis=2)
    return jnp.sum(matrices[:, :, :, None] * grid_field[:, :, None, :], axis=1)


def vertical_mix(matrix, grid_field):
    return jnp.dot(matrix, grid_field.reshape(LEV, -1), precision=HIGHEST).reshape(grid_field.shape)


def total(vals, axes=("lat", "lon")):
    v = jnp.stack(vals)
    for axis in axes:
        n = lax.axis_size(axis)
        g = lax.all_to_all(jnp.broadcast_to(v[None], (n,) + v.shape), axis, 0, 0, tiled=True)
        v = jnp.sum(g, axis=0)
    return tuple(v[i] for i in range(len(vals)))


def local(iterate, residual, direction, obs_weight, vertical, lon_taps, lat_taps, band_sizes):
    bounds = jnp.cumsum(band_sizes)
    levels = jnp.arange(LEV, dtype=jnp.int32)
    groups = jnp.sum((levels[:, None] >= bounds[None, :]).astype(jnp.int32), axis=1)
    lon_part = lon_pass(direction, lon_taps, groups, False)
    both = to_columns(jnp.concatenate([lon_part, obs_weight], axis=0))
    lat_width = both.shape[1]
    matrices = band_matrices(group_rows(groups, lat_taps), lat_width, lat_width)
    lat_part = lat_pass(both[:LEV], matrices, False)
    lifted = vertical_mix(vertical, lat_part)
    weighted = both[LEV:] * lifted
    partial = jnp.stack(
        [jnp.sum(residual * residual), jnp.sum(direction * direction) + jnp.sum(weighted * lifted)]
    )
    back_vert = vertical_mix(vertical.T, weighted)
    back_cols = lat_pass(back_vert, matrices, True)
    chunk = back_cols.shape[2]
    extra = jnp.zeros((1,) + back_cols.shape[1:], back_cols.dtype).at[0, :, :2].set(partial)
    returned = to_rows(jnp.concatenate([back_cols, extra], axis=0))
    back_lat = returned[:LEV]
    lat_sums = jnp.sum(returned[LEV, 0].reshape(-1, chunk)[:, :2], axis=0)
    norm_old, curvature = total((lat_sums[0], lat_sums[1]), ("lon",))
    applied = lax.optimization_barrier(direction + lon_pass(back_lat, lon_taps, groups, True))
    step_length = norm_old / curvature
    residual_next = residual - step_length * applied
    (norm_new,) = total((jnp.sum(residual_next * residual_next),), ("lon", "lat"))
    iterate_next = iterate + step_length * direction
    direction_next = residual_next + norm_new / norm_old * direction
    return (iterate_next, residual_next, direction_next)


def solution(mesh):
    placed = (
        P(None, "lat", "lon"),
        P(None, "lat", "lon"),
        P(None, "lat", "lon"),
        P(None, "lat", "lon"),
        P(),
        P(),
        P(),
        P(),
    )
    return jax.shard_map(
        local,
        mesh=mesh,
        in_specs=placed,
        out_specs=(P(None, "lat", "lon"), P(None, "lat", "lon"), P(None, "lat", "lon")),
        check_vma=False,
    )
```

```python
import jax
import jax.numpy as jnp
from jax import lax
from jax.experimental import pallas as pl
from jax.sharding import PartitionSpec as P

LEV = 127
TAPS = 101
HALF = 50
GROUPS = 32


HIGHEST = lax.Precision.HIGHEST


def with_halo(cells, sides, width):
    for axis, dim in sides:
        count = lax.axis_size(axis)
        head = lax.slice_in_dim(cells, 0, width, axis=dim)
        tail = lax.slice_in_dim(cells, cells.shape[dim] - width, cells.shape[dim], axis=dim)
        cells = jnp.concatenate(
            [
                lax.ppermute(tail, axis, [(i, (i + 1) % count) for i in range(count)]),
                cells,
                lax.ppermute(head, axis, [((i + 1) % count, i) for i in range(count)]),
            ],
            axis=dim,
        )
    return cells


def band_matrices(kernel, width_in, width_out):
    offsets = (
        jnp.arange(width_in, dtype=jnp.int32)[:, None]
        - jnp.arange(width_out, dtype=jnp.int32)[None, :]
        + HALF
    )
    inside = (offsets >= 0) & (offsets < TAPS)
    picked = kernel[:, jnp.clip(offsets, 0, TAPS - 1)]
    return jnp.where(inside[None], picked, jnp.zeros_like(picked))


def group_rows(group_ids, kernel):
    onehot = (group_ids[:, None] == jnp.arange(GROUPS, dtype=jnp.int32)[None, :]).astype(
        jnp.float32
    )
    return jnp.dot(onehot, kernel, precision=HIGHEST)


def slot_plan(groups, devices_count):
    levels = jnp.arange(LEV, dtype=jnp.int32)
    capacity = (LEV + devices_count - 1) // devices_count
    slot_ids = jnp.arange(devices_count * capacity, dtype=jnp.int32)
    matched = levels[None, :] == slot_ids[:, None]
    occupied = jnp.any(matched, axis=1)
    sources = jnp.sum(jnp.where(matched, levels[None, :], 0), axis=1)
    sources = jnp.where(occupied, sources, LEV)
    slot_groups = jnp.sum(jnp.where(matched, groups[None, :], 0), axis=1)
    return (capacity, levels, sources, slot_groups)


def into_slots(grid_field, sources):
    padded = jnp.concatenate(
        [grid_field, jnp.zeros((1,) + grid_field.shape[1:], grid_field.dtype)], axis=0
    )
    return jnp.take(padded, sources, axis=0)


def lon_kernel(taps_ref, extended_ref, out_ref):
    width = out_ref.shape[0]
    total_sum = taps_ref[0:1, :] * extended_ref[0:width, :]
    for shift_tap in range(1, TAPS):
        total_sum = total_sum + taps_ref[shift_tap : shift_tap + 1, :] * extended_ref[
            shift_tap : shift_tap + width, :
        ]
    out_ref[...] = total_sum


def lon_pass(grid_field, taps_t, adjoint):
    taps_t = taps_t[::-1] if adjoint else taps_t
    levels, rows, lon_width = grid_field.shape
    extended = with_halo(grid_field, (("lon", 2),), HALF)
    filtered = pl.pallas_call(
        lon_kernel, out_shape=jax.ShapeDtypeStruct((lon_width, levels * rows), grid_field.dtype)
    )(taps_t, extended.reshape(levels * rows, -1).T)
    return filtered.T.reshape(levels, rows, lon_width)


def to_columns(grid_field):
    return lax.all_to_all(grid_field, "lat", 2, 1, tiled=True)


def to_rows(grid_field):
    return lax.all_to_all(grid_field, "lat", 1, 2, tiled=True)


def lat_pass(grid_field, matrices, adjoint):
    if adjoint:
        return jnp.sum(matrices[:, :, :, None] * grid_field[:, None, :, :], axis=2)
    return jnp.sum(matrices[:, :, :, None] * grid_field[:, :, None, :], axis=1)


def vertical_mix(matrix, grid_field):
    return jnp.dot(matrix, grid_field.reshape(LEV, -1), precision=HIGHEST).reshape(grid_field.shape)


def total(vals, axes=("lat", "lon")):
    v = jnp.stack(vals)
    for axis in axes:
        n = lax.axis_size(axis)
        g = lax.all_to_all(jnp.broadcast_to(v[None], (n,) + v.shape), axis, 0, 0, tiled=True)
        v = jnp.sum(g, axis=0)
    return tuple(v[i] for i in range(len(vals)))


def local(iterate, residual, direction, obs_weight, vertical, lon_taps, lat_taps, band_sizes):
    bounds = jnp.cumsum(band_sizes)
    levels = jnp.arange(LEV, dtype=jnp.int32)
    groups = jnp.sum((levels[:, None] >= bounds[None, :]).astype(jnp.int32), axis=1)
    rows = direction.shape[1]
    lon_t = jnp.repeat(group_rows(groups, lon_taps), rows, axis=0).T
    lon_part = lon_pass(direction, lon_t, False)
    both = to_columns(jnp.concatenate([lon_part, obs_weight], axis=0))
    lat_width = both.shape[1]
    matrices = band_matrices(group_rows(groups, lat_taps), lat_width, lat_width)
    lat_part = lat_pass(both[:LEV], matrices, False)
    lifted = vertical_mix(vertical, lat_part)
    weighted = both[LEV:] * lifted
    partial = jnp.stack(
        [jnp.sum(residual * residual), jnp.sum(direction * direction) + jnp.sum(weighted * lifted)]
    )
    back_vert = vertical_mix(vertical.T, weighted)
    back_cols = lat_pass(back_vert, matrices, True)
    chunk = back_cols.shape[2]
    extra = jnp.zeros((1,) + back_cols.shape[1:], back_cols.dtype).at[0, :, :2].set(partial)
    returned = to_rows(jnp.concatenate([back_cols, extra], axis=0))
    back_lat = returned[:LEV]
    lat_sums = jnp.sum(returned[LEV, 0].reshape(-1, chunk)[:, :2], axis=0)
    norm_old, curvature = total((lat_sums[0], lat_sums[1]), ("lon",))
    applied = lax.optimization_barrier(direction + lon_pass(back_lat, lon_t, True))
    step_length = norm_old / curvature
    residual_next = residual - step_length * applied
    (norm_new,) = total((jnp.sum(residual_next * residual_next),), ("lon", "lat"))
    iterate_next = iterate + step_length * direction
    direction_next = residual_next + norm_new / norm_old * direction
    return (iterate_next, residual_next, direction_next)


def solution(mesh):
    placed = (
        P(None, "lat", "lon"),
        P(None, "lat", "lon"),
        P(None, "lat", "lon"),
        P(None, "lat", "lon"),
        P(),
        P(),
        P(),
        P(),
    )
    return jax.shard_map(
        local,
        mesh=mesh,
        in_specs=placed,
        out_specs=(P(None, "lat", "lon"), P(None, "lat", "lon"), P(None, "lat", "lon")),
        check_vma=False,
    )
```

```python
import jax
import jax.numpy as jnp
from jax import lax
from jax.experimental import pallas as pl
from jax.sharding import PartitionSpec as P

LEV = 127
TAPS = 101
HALF = 50
GROUPS = 32


HIGHEST = lax.Precision.HIGHEST


def with_halo(cells, sides, width):
    for axis, dim in sides:
        count = lax.axis_size(axis)
        head = lax.slice_in_dim(cells, 0, width, axis=dim)
        tail = lax.slice_in_dim(cells, cells.shape[dim] - width, cells.shape[dim], axis=dim)
        cells = jnp.concatenate(
            [
                lax.ppermute(tail, axis, [(i, (i + 1) % count) for i in range(count)]),
                cells,
                lax.ppermute(head, axis, [((i + 1) % count, i) for i in range(count)]),
            ],
            axis=dim,
        )
    return cells


def band_matrices(kernel, width_in, width_out):
    offsets = (
        jnp.arange(width_in, dtype=jnp.int32)[:, None]
        - jnp.arange(width_out, dtype=jnp.int32)[None, :]
        + HALF
    )
    inside = (offsets >= 0) & (offsets < TAPS)
    picked = kernel[:, jnp.clip(offsets, 0, TAPS - 1)]
    return jnp.where(inside[None], picked, jnp.zeros_like(picked))


def group_rows(group_ids, kernel):
    onehot = (group_ids[:, None] == jnp.arange(GROUPS, dtype=jnp.int32)[None, :]).astype(
        jnp.float32
    )
    return jnp.dot(onehot, kernel, precision=HIGHEST)


def slot_plan(groups, devices_count):
    levels = jnp.arange(LEV, dtype=jnp.int32)
    capacity = (LEV + devices_count - 1) // devices_count
    slot_ids = jnp.arange(devices_count * capacity, dtype=jnp.int32)
    matched = levels[None, :] == slot_ids[:, None]
    occupied = jnp.any(matched, axis=1)
    sources = jnp.sum(jnp.where(matched, levels[None, :], 0), axis=1)
    sources = jnp.where(occupied, sources, LEV)
    slot_groups = jnp.sum(jnp.where(matched, groups[None, :], 0), axis=1)
    return (capacity, levels, sources, slot_groups)


def into_slots(grid_field, sources):
    padded = jnp.concatenate(
        [grid_field, jnp.zeros((1,) + grid_field.shape[1:], grid_field.dtype)], axis=0
    )
    return jnp.take(padded, sources, axis=0)


def lon_kernel(taps_ref, extended_ref, out_ref):
    width = out_ref.shape[0]
    total_sum = taps_ref[0:1, :] * extended_ref[0:width, :]
    for shift_tap in range(1, TAPS):
        total_sum = total_sum + taps_ref[shift_tap : shift_tap + 1, :] * extended_ref[
            shift_tap : shift_tap + width, :
        ]
    out_ref[...] = total_sum


def lon_add_kernel(taps_ref, extended_ref, base_ref, out_ref):
    width = out_ref.shape[1]
    total_sum = taps_ref[0:1, :] * extended_ref[0:width, :]
    for shift_tap in range(1, TAPS):
        total_sum = total_sum + taps_ref[shift_tap : shift_tap + 1, :] * extended_ref[
            shift_tap : shift_tap + width, :
        ]
    out_ref[...] = base_ref[...] + total_sum.T


def lon_pass_add(grid_field, base, kernel_groups, groups):
    kernel = kernel_groups[:, ::-1]
    levels, rows, lon_width = grid_field.shape
    kernels = jnp.repeat(group_rows(groups, kernel), rows, axis=0)
    extended = with_halo(grid_field, (("lon", 2),), HALF)
    filtered = pl.pallas_call(
        lon_add_kernel,
        out_shape=jax.ShapeDtypeStruct((levels * rows, lon_width), grid_field.dtype),
    )(kernels.T, extended.reshape(levels * rows, -1).T, base.reshape(levels * rows, lon_width))
    return filtered.reshape(levels, rows, lon_width)


def lon_pass(grid_field, kernel_groups, groups, adjoint):
    kernel = kernel_groups[:, ::-1] if adjoint else kernel_groups
    levels, rows, lon_width = grid_field.shape
    kernels = jnp.repeat(group_rows(groups, kernel), rows, axis=0)
    extended = with_halo(grid_field, (("lon", 2),), HALF)
    filtered = pl.pallas_call(
        lon_kernel, out_shape=jax.ShapeDtypeStruct((lon_width, levels * rows), grid_field.dtype)
    )(kernels.T, extended.reshape(levels * rows, -1).T)
    return filtered.T.reshape(levels, rows, lon_width)


def to_columns(grid_field):
    return lax.all_to_all(grid_field, "lat", 2, 1, tiled=True)


def to_rows(grid_field):
    return lax.all_to_all(grid_field, "lat", 1, 2, tiled=True)


def lat_pass(grid_field, matrices, adjoint):
    if adjoint:
        return jnp.sum(matrices[:, :, :, None] * grid_field[:, None, :, :], axis=2)
    return jnp.sum(matrices[:, :, :, None] * grid_field[:, :, None, :], axis=1)


def vertical_mix(matrix, grid_field):
    return jnp.dot(matrix, grid_field.reshape(LEV, -1), precision=HIGHEST).reshape(grid_field.shape)


def total(vals, axes=("lat", "lon")):
    v = jnp.stack(vals)
    for axis in axes:
        n = lax.axis_size(axis)
        g = lax.all_to_all(jnp.broadcast_to(v[None], (n,) + v.shape), axis, 0, 0, tiled=True)
        v = jnp.sum(g, axis=0)
    return tuple(v[i] for i in range(len(vals)))


def local(iterate, residual, direction, obs_weight, vertical, lon_taps, lat_taps, band_sizes):
    bounds = jnp.cumsum(band_sizes)
    levels = jnp.arange(LEV, dtype=jnp.int32)
    groups = jnp.sum((levels[:, None] >= bounds[None, :]).astype(jnp.int32), axis=1)
    lon_part = lon_pass(direction, lon_taps, groups, False)
    both = to_columns(jnp.concatenate([lon_part, obs_weight], axis=0))
    lat_width = both.shape[1]
    matrices = band_matrices(group_rows(groups, lat_taps), lat_width, lat_width)
    lat_part = lat_pass(both[:LEV], matrices, False)
    lifted = vertical_mix(vertical, lat_part)
    weighted = both[LEV:] * lifted
    partial = jnp.stack(
        [jnp.sum(residual * residual), jnp.sum(direction * direction) + jnp.sum(weighted * lifted)]
    )
    back_vert = vertical_mix(vertical.T, weighted)
    back_cols = lat_pass(back_vert, matrices, True)
    chunk = back_cols.shape[2]
    extra = jnp.zeros((1,) + back_cols.shape[1:], back_cols.dtype).at[0, :, :2].set(partial)
    returned = to_rows(jnp.concatenate([back_cols, extra], axis=0))
    back_lat = returned[:LEV]
    lat_sums = jnp.sum(returned[LEV, 0].reshape(-1, chunk)[:, :2], axis=0)
    norm_old, curvature = total((lat_sums[0], lat_sums[1]), ("lon",))
    applied = lon_pass_add(back_lat, direction, lon_taps, groups)
    step_length = norm_old / curvature
    residual_next = residual - step_length * applied
    (norm_new,) = total((jnp.sum(residual_next * residual_next),))
    iterate_next = iterate + step_length * direction
    direction_next = residual_next + norm_new / norm_old * direction
    return (iterate_next, residual_next, direction_next)


def solution(mesh):
    placed = (
        P(None, "lat", "lon"),
        P(None, "lat", "lon"),
        P(None, "lat", "lon"),
        P(None, "lat", "lon"),
        P(),
        P(),
        P(),
        P(),
    )
    return jax.shard_map(
        local,
        mesh=mesh,
        in_specs=placed,
        out_specs=(P(None, "lat", "lon"), P(None, "lat", "lon"), P(None, "lat", "lon")),
        check_vma=False,
    )
```

```python
import jax
import jax.numpy as jnp
from jax import lax
from jax.experimental import pallas as pl
from jax.sharding import PartitionSpec as P

LEV = 127
TAPS = 101
HALF = 50
GROUPS = 32


HIGHEST = lax.Precision.HIGHEST


def with_halo(cells, sides, width):
    for axis, dim in sides:
        count = lax.axis_size(axis)
        head = lax.slice_in_dim(cells, 0, width, axis=dim)
        tail = lax.slice_in_dim(cells, cells.shape[dim] - width, cells.shape[dim], axis=dim)
        cells = jnp.concatenate(
            [
                lax.ppermute(tail, axis, [(i, (i + 1) % count) for i in range(count)]),
                cells,
                lax.ppermute(head, axis, [((i + 1) % count, i) for i in range(count)]),
            ],
            axis=dim,
        )
    return cells


def band_matrices(kernel, width_in, width_out):
    offsets = (
        jnp.arange(width_in, dtype=jnp.int32)[:, None]
        - jnp.arange(width_out, dtype=jnp.int32)[None, :]
        + HALF
    )
    inside = (offsets >= 0) & (offsets < TAPS)
    picked = kernel[:, jnp.clip(offsets, 0, TAPS - 1)]
    return jnp.where(inside[None], picked, jnp.zeros_like(picked))


def group_rows(group_ids, kernel):
    onehot = (group_ids[:, None] == jnp.arange(GROUPS, dtype=jnp.int32)[None, :]).astype(
        jnp.float32
    )
    return jnp.dot(onehot, kernel, precision=HIGHEST)


def slot_plan(groups, devices_count):
    levels = jnp.arange(LEV, dtype=jnp.int32)
    capacity = (LEV + devices_count - 1) // devices_count
    slot_ids = jnp.arange(devices_count * capacity, dtype=jnp.int32)
    matched = levels[None, :] == slot_ids[:, None]
    occupied = jnp.any(matched, axis=1)
    sources = jnp.sum(jnp.where(matched, levels[None, :], 0), axis=1)
    sources = jnp.where(occupied, sources, LEV)
    slot_groups = jnp.sum(jnp.where(matched, groups[None, :], 0), axis=1)
    return (capacity, levels, sources, slot_groups)


def into_slots(grid_field, sources):
    padded = jnp.concatenate(
        [grid_field, jnp.zeros((1,) + grid_field.shape[1:], grid_field.dtype)], axis=0
    )
    return jnp.take(padded, sources, axis=0)


def lon_kernel(taps_ref, extended_ref, out_ref):
    width = out_ref.shape[1]
    total_sum = taps_ref[0:1, :] * extended_ref[0:width, :]
    for shift_tap in range(1, TAPS):
        total_sum = total_sum + taps_ref[shift_tap : shift_tap + 1, :] * extended_ref[
            shift_tap : shift_tap + width, :
        ]
    out_ref[...] = total_sum.T


def lon_add_kernel(taps_ref, extended_ref, base_ref, out_ref):
    width = out_ref.shape[1]
    total_sum = taps_ref[0:1, :] * extended_ref[0:width, :]
    for shift_tap in range(1, TAPS):
        total_sum = total_sum + taps_ref[shift_tap : shift_tap + 1, :] * extended_ref[
            shift_tap : shift_tap + width, :
        ]
    out_ref[...] = base_ref[...] + total_sum.T


def lon_pass_add(grid_field, base, kernel_groups, groups):
    kernel = kernel_groups[:, ::-1]
    levels, rows, lon_width = grid_field.shape
    kernels = jnp.repeat(group_rows(groups, kernel), rows, axis=0)
    extended = with_halo(grid_field, (("lon", 2),), HALF)
    filtered = pl.pallas_call(
        lon_add_kernel,
        out_shape=jax.ShapeDtypeStruct((levels * rows, lon_width), grid_field.dtype),
    )(kernels.T, extended.reshape(levels * rows, -1).T, base.reshape(levels * rows, lon_width))
    return filtered.reshape(levels, rows, lon_width)


def lon_pass(grid_field, kernel_groups, groups, adjoint):
    kernel = kernel_groups[:, ::-1] if adjoint else kernel_groups
    levels, rows, lon_width = grid_field.shape
    kernels = jnp.repeat(group_rows(groups, kernel), rows, axis=0)
    extended = with_halo(grid_field, (("lon", 2),), HALF)
    filtered = pl.pallas_call(
        lon_kernel, out_shape=jax.ShapeDtypeStruct((levels * rows, lon_width), grid_field.dtype)
    )(kernels.T, extended.reshape(levels * rows, -1).T)
    return filtered.reshape(levels, rows, lon_width)


def to_columns(grid_field):
    return lax.all_to_all(grid_field, "lat", 2, 1, tiled=True)


def to_rows(grid_field):
    return lax.all_to_all(grid_field, "lat", 1, 2, tiled=True)


def lat_pass(grid_field, matrices, adjoint):
    if adjoint:
        return jnp.sum(matrices[:, :, :, None] * grid_field[:, None, :, :], axis=2)
    return jnp.sum(matrices[:, :, :, None] * grid_field[:, :, None, :], axis=1)


def vertical_mix(matrix, grid_field):
    return jnp.dot(matrix, grid_field.reshape(LEV, -1), precision=HIGHEST).reshape(grid_field.shape)


def total(vals, axes=("lat", "lon")):
    v = jnp.stack(vals)
    for axis in axes:
        n = lax.axis_size(axis)
        g = lax.all_to_all(jnp.broadcast_to(v[None], (n,) + v.shape), axis, 0, 0, tiled=True)
        v = jnp.sum(g, axis=0)
    return tuple(v[i] for i in range(len(vals)))


def local(iterate, residual, direction, obs_weight, vertical, lon_taps, lat_taps, band_sizes):
    bounds = jnp.cumsum(band_sizes)
    levels = jnp.arange(LEV, dtype=jnp.int32)
    groups = jnp.sum((levels[:, None] >= bounds[None, :]).astype(jnp.int32), axis=1)
    lon_part = lon_pass(direction, lon_taps, groups, False)
    both = to_columns(jnp.concatenate([lon_part, obs_weight], axis=0))
    lat_width = both.shape[1]
    matrices = band_matrices(group_rows(groups, lat_taps), lat_width, lat_width)
    lat_part = lat_pass(both[:LEV], matrices, False)
    lifted = vertical_mix(vertical, lat_part)
    weighted = both[LEV:] * lifted
    partial = jnp.stack(
        [jnp.sum(residual * residual), jnp.sum(direction * direction) + jnp.sum(weighted * lifted)]
    )
    back_vert = vertical_mix(vertical.T, weighted)
    back_cols = lat_pass(back_vert, matrices, True)
    chunk = back_cols.shape[2]
    extra = jnp.zeros((1,) + back_cols.shape[1:], back_cols.dtype).at[0, :, :2].set(partial)
    returned = to_rows(jnp.concatenate([back_cols, extra], axis=0))
    back_lat = returned[:LEV]
    lat_sums = jnp.sum(returned[LEV, 0].reshape(-1, chunk)[:, :2], axis=0)
    norm_old, curvature = total((lat_sums[0], lat_sums[1]), ("lon",))
    applied = lon_pass_add(back_lat, direction, lon_taps, groups)
    step_length = norm_old / curvature
    residual_next = residual - step_length * applied
    (norm_new,) = total((jnp.sum(residual_next * residual_next),))
    iterate_next = iterate + step_length * direction
    direction_next = residual_next + norm_new / norm_old * direction
    return (iterate_next, residual_next, direction_next)


def solution(mesh):
    placed = (
        P(None, "lat", "lon"),
        P(None, "lat", "lon"),
        P(None, "lat", "lon"),
        P(None, "lat", "lon"),
        P(),
        P(),
        P(),
        P(),
    )
    return jax.shard_map(
        local,
        mesh=mesh,
        in_specs=placed,
        out_specs=(P(None, "lat", "lon"), P(None, "lat", "lon"), P(None, "lat", "lon")),
        check_vma=False,
    )
```

```python
import jax
import jax.numpy as jnp
from jax import lax
from jax.experimental import pallas as pl
from jax.sharding import PartitionSpec as P

LEV = 127
TAPS = 101
HALF = 50
GROUPS = 32


HIGHEST = lax.Precision.HIGHEST


def with_halo(cells, sides, width):
    for axis, dim in sides:
        count = lax.axis_size(axis)
        head = lax.slice_in_dim(cells, 0, width, axis=dim)
        tail = lax.slice_in_dim(cells, cells.shape[dim] - width, cells.shape[dim], axis=dim)
        cells = jnp.concatenate(
            [
                lax.ppermute(tail, axis, [(i, (i + 1) % count) for i in range(count)]),
                cells,
                lax.ppermute(head, axis, [((i + 1) % count, i) for i in range(count)]),
            ],
            axis=dim,
        )
    return cells


def band_matrices(kernel, width_in, width_out):
    offsets = (
        jnp.arange(width_in, dtype=jnp.int32)[:, None]
        - jnp.arange(width_out, dtype=jnp.int32)[None, :]
        + HALF
    )
    inside = (offsets >= 0) & (offsets < TAPS)
    picked = kernel[:, jnp.clip(offsets, 0, TAPS - 1)]
    return jnp.where(inside[None], picked, jnp.zeros_like(picked))


def group_rows(group_ids, kernel):
    onehot = (group_ids[:, None] == jnp.arange(GROUPS, dtype=jnp.int32)[None, :]).astype(
        jnp.float32
    )
    return jnp.dot(onehot, kernel, precision=HIGHEST)


def slot_plan(groups, devices_count):
    levels = jnp.arange(LEV, dtype=jnp.int32)
    capacity = (LEV + devices_count - 1) // devices_count
    slot_ids = jnp.arange(devices_count * capacity, dtype=jnp.int32)
    matched = levels[None, :] == slot_ids[:, None]
    occupied = jnp.any(matched, axis=1)
    sources = jnp.sum(jnp.where(matched, levels[None, :], 0), axis=1)
    sources = jnp.where(occupied, sources, LEV)
    slot_groups = jnp.sum(jnp.where(matched, groups[None, :], 0), axis=1)
    return (capacity, levels, sources, slot_groups)


def into_slots(grid_field, sources):
    padded = jnp.concatenate(
        [grid_field, jnp.zeros((1,) + grid_field.shape[1:], grid_field.dtype)], axis=0
    )
    return jnp.take(padded, sources, axis=0)


def lon_kernel(taps_ref, extended_ref, out_ref):
    width = out_ref.shape[0]
    total_sum = taps_ref[0:1, :] * extended_ref[0:width, :]
    for shift_tap in range(1, TAPS):
        total_sum = total_sum + taps_ref[shift_tap : shift_tap + 1, :] * extended_ref[
            shift_tap : shift_tap + width, :
        ]
    out_ref[...] = total_sum


def lon_add_kernel(taps_ref, extended_ref, base_ref, out_ref):
    width = out_ref.shape[1]
    total_sum = taps_ref[0:1, :] * extended_ref[0:width, :]
    for shift_tap in range(1, TAPS):
        total_sum = total_sum + taps_ref[shift_tap : shift_tap + 1, :] * extended_ref[
            shift_tap : shift_tap + width, :
        ]
    out_ref[...] = base_ref[...] + total_sum.T


def lon_pass_add(grid_field, base, kernel_groups, groups):
    kernel = kernel_groups[:, ::-1]
    levels, rows, lon_width = grid_field.shape
    kernels = jnp.repeat(group_rows(groups, kernel), rows, axis=0)
    extended = with_halo(grid_field, (("lon", 2),), HALF)
    filtered = pl.pallas_call(
        lon_add_kernel,
        out_shape=jax.ShapeDtypeStruct((levels * rows, lon_width), grid_field.dtype),
    )(kernels.T, extended.reshape(levels * rows, -1).T, base.reshape(levels * rows, lon_width))
    return filtered.reshape(levels, rows, lon_width)


def lon_pass(grid_field, kernel_groups, groups, adjoint):
    kernel = kernel_groups[:, ::-1] if adjoint else kernel_groups
    levels, rows, lon_width = grid_field.shape
    kernels = jnp.repeat(group_rows(groups, kernel), rows, axis=0)
    extended = with_halo(grid_field, (("lon", 2),), HALF)
    filtered = pl.pallas_call(
        lon_kernel, out_shape=jax.ShapeDtypeStruct((lon_width, levels * rows), grid_field.dtype)
    )(kernels.T, extended.reshape(levels * rows, -1).T)
    return filtered.T.reshape(levels, rows, lon_width)


def to_columns(grid_field):
    return lax.all_to_all(grid_field, "lat", 2, 1, tiled=True)


def to_rows(grid_field):
    return lax.all_to_all(grid_field, "lat", 1, 2, tiled=True)


def lat_pass(grid_field, matrices, adjoint):
    if adjoint:
        return jnp.sum(matrices[:, :, :, None] * grid_field[:, None, :, :], axis=2)
    return jnp.sum(matrices[:, :, :, None] * grid_field[:, :, None, :], axis=1)


def vertical_mix(matrix, grid_field):
    return jnp.dot(matrix, grid_field.reshape(LEV, -1), precision=HIGHEST).reshape(grid_field.shape)


def total(vals, axes=("lat", "lon")):
    v = jnp.stack(vals)
    for axis in axes:
        n = lax.axis_size(axis)
        g = lax.all_to_all(jnp.broadcast_to(v[None], (n,) + v.shape), axis, 0, 0, tiled=True)
        v = jnp.sum(g, axis=0)
    return tuple(v[i] for i in range(len(vals)))


def local(iterate, residual, direction, obs_weight, vertical, lon_taps, lat_taps, band_sizes):
    bounds = jnp.cumsum(band_sizes)
    levels = jnp.arange(LEV, dtype=jnp.int32)
    groups = jnp.sum((levels[:, None] >= bounds[None, :]).astype(jnp.int32), axis=1)
    lon_part = lon_pass(direction, lon_taps, groups, False)
    both = to_columns(jnp.concatenate([lon_part, obs_weight], axis=0))
    lat_width = both.shape[1]
    matrices = band_matrices(group_rows(groups, lat_taps), lat_width, lat_width)
    lat_part = lat_pass(both[:LEV], matrices, False)
    lifted = vertical_mix(vertical, lat_part)
    weighted = both[LEV:] * lifted
    partial = jnp.stack(
        [jnp.sum(residual * residual), jnp.sum(direction * direction) + jnp.sum(weighted * lifted)]
    )
    back_vert = vertical_mix(vertical.T, weighted)
    back_cols = lat_pass(back_vert, matrices, True)
    chunk = back_cols.shape[2]
    extra = jnp.zeros((1,) + back_cols.shape[1:], back_cols.dtype).at[0, :, :2].set(partial)
    returned = to_rows(jnp.concatenate([back_cols, extra], axis=0))
    back_lat = returned[:LEV]
    lat_sums = jnp.sum(returned[LEV, 0].reshape(-1, chunk)[:, :2], axis=0)
    norm_old, curvature = total((lat_sums[0], lat_sums[1]), ("lon",))
    applied = lon_pass_add(back_lat, direction, lon_taps, groups)
    step_length = norm_old / curvature
    residual_next = residual - step_length * applied
    (norm_new,) = total((jnp.sum(residual_next * residual_next),), ("lon", "lat"))
    iterate_next = iterate + step_length * direction
    direction_next = residual_next + norm_new / norm_old * direction
    return (iterate_next, residual_next, direction_next)


def solution(mesh):
    placed = (
        P(None, "lat", "lon"),
        P(None, "lat", "lon"),
        P(None, "lat", "lon"),
        P(None, "lat", "lon"),
        P(),
        P(),
        P(),
        P(),
    )
    return jax.shard_map(
        local,
        mesh=mesh,
        in_specs=placed,
        out_specs=(P(None, "lat", "lon"), P(None, "lat", "lon"), P(None, "lat", "lon")),
        check_vma=False,
    )
```

```python
import jax
import jax.numpy as jnp
from jax import lax
from jax.experimental import pallas as pl
from jax.sharding import PartitionSpec as P

LEV = 127
TAPS = 101
HALF = 50
GROUPS = 32


HIGHEST = lax.Precision.HIGHEST


def with_halo(cells, sides, width):
    for axis, dim in sides:
        count = lax.axis_size(axis)
        head = lax.slice_in_dim(cells, 0, width, axis=dim)
        tail = lax.slice_in_dim(cells, cells.shape[dim] - width, cells.shape[dim], axis=dim)
        cells = jnp.concatenate(
            [
                lax.ppermute(tail, axis, [(i, (i + 1) % count) for i in range(count)]),
                cells,
                lax.ppermute(head, axis, [((i + 1) % count, i) for i in range(count)]),
            ],
            axis=dim,
        )
    return cells


def band_matrices(kernel, width_in, width_out):
    offsets = (
        jnp.arange(width_in, dtype=jnp.int32)[:, None]
        - jnp.arange(width_out, dtype=jnp.int32)[None, :]
        + HALF
    )
    inside = (offsets >= 0) & (offsets < TAPS)
    picked = kernel[:, jnp.clip(offsets, 0, TAPS - 1)]
    return jnp.where(inside[None], picked, jnp.zeros_like(picked))


def group_rows(group_ids, kernel):
    onehot = (group_ids[:, None] == jnp.arange(GROUPS, dtype=jnp.int32)[None, :]).astype(
        jnp.float32
    )
    return jnp.dot(onehot, kernel, precision=HIGHEST)


def slot_plan(groups, devices_count):
    levels = jnp.arange(LEV, dtype=jnp.int32)
    capacity = (LEV + devices_count - 1) // devices_count
    slot_ids = jnp.arange(devices_count * capacity, dtype=jnp.int32)
    matched = levels[None, :] == slot_ids[:, None]
    occupied = jnp.any(matched, axis=1)
    sources = jnp.sum(jnp.where(matched, levels[None, :], 0), axis=1)
    sources = jnp.where(occupied, sources, LEV)
    slot_groups = jnp.sum(jnp.where(matched, groups[None, :], 0), axis=1)
    return (capacity, levels, sources, slot_groups)


def into_slots(grid_field, sources):
    padded = jnp.concatenate(
        [grid_field, jnp.zeros((1,) + grid_field.shape[1:], grid_field.dtype)], axis=0
    )
    return jnp.take(padded, sources, axis=0)


def lon_kernel(taps_ref, extended_ref, out_ref):
    width = out_ref.shape[0]
    total_sum = taps_ref[0:1, :] * extended_ref[0:width, :]
    for shift_tap in range(1, TAPS):
        total_sum = total_sum + taps_ref[shift_tap : shift_tap + 1, :] * extended_ref[
            shift_tap : shift_tap + width, :
        ]
    out_ref[...] = total_sum


def lon_add_kernel(taps_ref, extended_ref, base_ref, out_ref):
    width = out_ref.shape[1]
    total_sum = taps_ref[0:1, :] * extended_ref[0:width, :]
    for shift_tap in range(1, TAPS):
        total_sum = total_sum + taps_ref[shift_tap : shift_tap + 1, :] * extended_ref[
            shift_tap : shift_tap + width, :
        ]
    out_ref[...] = base_ref[...] + total_sum.T


def lon_pass_add(grid_field, base, kernels):
    kernels = kernels[:, ::-1]
    levels, rows, lon_width = grid_field.shape
    extended = with_halo(grid_field, (("lon", 2),), HALF)
    filtered = pl.pallas_call(
        lon_add_kernel,
        out_shape=jax.ShapeDtypeStruct((levels * rows, lon_width), grid_field.dtype),
    )(kernels.T, extended.reshape(levels * rows, -1).T, base.reshape(levels * rows, lon_width))
    return filtered.reshape(levels, rows, lon_width)


def lon_pass(grid_field, kernel_groups, groups, adjoint):
    kernel = kernel_groups[:, ::-1] if adjoint else kernel_groups
    levels, rows, lon_width = grid_field.shape
    kernels = jnp.repeat(group_rows(groups, kernel), rows, axis=0)
    extended = with_halo(grid_field, (("lon", 2),), HALF)
    filtered = pl.pallas_call(
        lon_kernel, out_shape=jax.ShapeDtypeStruct((lon_width, levels * rows), grid_field.dtype)
    )(kernels.T, extended.reshape(levels * rows, -1).T)
    return filtered.T.reshape(levels, rows, lon_width)


def to_columns(grid_field):
    return lax.all_to_all(grid_field, "lat", 2, 1, tiled=True)


def to_rows(grid_field):
    return lax.all_to_all(grid_field, "lat", 1, 2, tiled=True)


def lat_pass(grid_field, matrices, adjoint):
    if adjoint:
        return jnp.sum(matrices[:, :, :, None] * grid_field[:, None, :, :], axis=2)
    return jnp.sum(matrices[:, :, :, None] * grid_field[:, :, None, :], axis=1)


def vertical_mix(matrix, grid_field):
    return jnp.dot(matrix, grid_field.reshape(LEV, -1), precision=HIGHEST).reshape(grid_field.shape)


def total(vals, axes=("lat", "lon")):
    v = jnp.stack(vals)
    for axis in axes:
        n = lax.axis_size(axis)
        g = lax.all_to_all(jnp.broadcast_to(v[None], (n,) + v.shape), axis, 0, 0, tiled=True)
        v = jnp.sum(g, axis=0)
    return tuple(v[i] for i in range(len(vals)))


def local(iterate, residual, direction, obs_weight, vertical, lon_taps, lat_taps, band_sizes):
    bounds = jnp.cumsum(band_sizes)
    levels = jnp.arange(LEV, dtype=jnp.int32)
    groups = jnp.sum((levels[:, None] >= bounds[None, :]).astype(jnp.int32), axis=1)
    lon_part = lon_pass(direction, lon_taps, groups, False)
    both = to_columns(jnp.concatenate([lon_part, obs_weight], axis=0))
    lat_width = both.shape[1]
    matrices = band_matrices(group_rows(groups, lat_taps), lat_width, lat_width)
    lat_part = lat_pass(both[:LEV], matrices, False)
    lifted = vertical_mix(vertical, lat_part)
    weighted = both[LEV:] * lifted
    partial = jnp.stack(
        [jnp.sum(residual * residual), jnp.sum(direction * direction) + jnp.sum(weighted * lifted)]
    )
    back_vert = vertical_mix(vertical.T, weighted)
    back_cols = lat_pass(back_vert, matrices, True)
    chunk = back_cols.shape[2]
    extra = jnp.zeros((1,) + back_cols.shape[1:], back_cols.dtype).at[0, :, :2].set(partial)
    returned = to_rows(jnp.concatenate([back_cols, extra], axis=0))
    back_lat = returned[:LEV]
    lat_sums = jnp.sum(returned[LEV, 0].reshape(-1, chunk)[:, :2], axis=0)
    norm_old, curvature = total((lat_sums[0], lat_sums[1]), ("lon",))
    applied = lon_pass_add(back_lat, direction, jnp.repeat(group_rows(groups, lon_taps), direction.shape[1], axis=0))
    step_length = norm_old / curvature
    residual_next = residual - step_length * applied
    (norm_new,) = total((jnp.sum(residual_next * residual_next),))
    iterate_next = iterate + step_length * direction
    direction_next = residual_next + norm_new / norm_old * direction
    return (iterate_next, residual_next, direction_next)


def solution(mesh):
    placed = (
        P(None, "lat", "lon"),
        P(None, "lat", "lon"),
        P(None, "lat", "lon"),
        P(None, "lat", "lon"),
        P(),
        P(),
        P(),
        P(),
    )
    return jax.shard_map(
        local,
        mesh=mesh,
        in_specs=placed,
        out_specs=(P(None, "lat", "lon"), P(None, "lat", "lon"), P(None, "lat", "lon")),
        check_vma=False,
    )
```

```python
import jax
import jax.numpy as jnp
from jax import lax
from jax.experimental import pallas as pl
from jax.experimental.pallas import tpu as pltpu
from jax.sharding import PartitionSpec as P

LEV = 127
TAPS = 101
HALF = 50
GROUPS = 32


HIGHEST = lax.Precision.HIGHEST


def with_halo(cells, sides, width):
    for axis, dim in sides:
        count = lax.axis_size(axis)
        head = lax.slice_in_dim(cells, 0, width, axis=dim)
        tail = lax.slice_in_dim(cells, cells.shape[dim] - width, cells.shape[dim], axis=dim)
        cells = jnp.concatenate(
            [
                lax.ppermute(tail, axis, [(i, (i + 1) % count) for i in range(count)]),
                cells,
                lax.ppermute(head, axis, [((i + 1) % count, i) for i in range(count)]),
            ],
            axis=dim,
        )
    return cells


def band_matrices(kernel, width_in, width_out):
    offsets = (
        jnp.arange(width_in, dtype=jnp.int32)[:, None]
        - jnp.arange(width_out, dtype=jnp.int32)[None, :]
        + HALF
    )
    inside = (offsets >= 0) & (offsets < TAPS)
    picked = kernel[:, jnp.clip(offsets, 0, TAPS - 1)]
    return jnp.where(inside[None], picked, jnp.zeros_like(picked))


def group_rows(group_ids, kernel):
    onehot = (group_ids[:, None] == jnp.arange(GROUPS, dtype=jnp.int32)[None, :]).astype(
        jnp.float32
    )
    return jnp.dot(onehot, kernel, precision=HIGHEST)


def slot_plan(groups, devices_count):
    levels = jnp.arange(LEV, dtype=jnp.int32)
    capacity = (LEV + devices_count - 1) // devices_count
    slot_ids = jnp.arange(devices_count * capacity, dtype=jnp.int32)
    matched = levels[None, :] == slot_ids[:, None]
    occupied = jnp.any(matched, axis=1)
    sources = jnp.sum(jnp.where(matched, levels[None, :], 0), axis=1)
    sources = jnp.where(occupied, sources, LEV)
    slot_groups = jnp.sum(jnp.where(matched, groups[None, :], 0), axis=1)
    return (capacity, levels, sources, slot_groups)


def into_slots(grid_field, sources):
    padded = jnp.concatenate(
        [grid_field, jnp.zeros((1,) + grid_field.shape[1:], grid_field.dtype)], axis=0
    )
    return jnp.take(padded, sources, axis=0)


def lon_kernel(taps_ref, extended_ref, out_ref):
    width = out_ref.shape[0]
    total_sum = taps_ref[0:1, :] * extended_ref[0:width, :]
    for shift_tap in range(1, TAPS):
        total_sum = total_sum + taps_ref[shift_tap : shift_tap + 1, :] * extended_ref[
            shift_tap : shift_tap + width, :
        ]
    out_ref[...] = total_sum


def lon_add_kernel(taps_ref, extended_ref, base_ref, out_ref):
    width = out_ref.shape[1]
    total_sum = taps_ref[0:1, :] * extended_ref[0:width, :]
    for shift_tap in range(1, TAPS):
        total_sum = total_sum + taps_ref[shift_tap : shift_tap + 1, :] * extended_ref[
            shift_tap : shift_tap + width, :
        ]
    out_ref[...] = base_ref[...] + total_sum.T


def lon_pass_add(grid_field, base, kernel_groups, groups):
    kernel = kernel_groups[:, ::-1]
    levels, rows, lon_width = grid_field.shape
    kernels = jnp.repeat(group_rows(groups, kernel), rows, axis=0)
    extended = with_halo(grid_field, (("lon", 2),), HALF)
    filtered = pl.pallas_call(
        lon_add_kernel,
        out_shape=jax.ShapeDtypeStruct((levels * rows, lon_width), grid_field.dtype),
    )(kernels.T, extended.reshape(levels * rows, -1).T, base.reshape(levels * rows, lon_width))
    return filtered.reshape(levels, rows, lon_width)


def lon_pass(grid_field, kernel_groups, groups, adjoint):
    kernel = kernel_groups[:, ::-1] if adjoint else kernel_groups
    levels, rows, lon_width = grid_field.shape
    kernels = jnp.repeat(group_rows(groups, kernel), rows, axis=0)
    extended = with_halo(grid_field, (("lon", 2),), HALF)
    filtered = pl.pallas_call(
        lon_kernel, out_shape=jax.ShapeDtypeStruct((lon_width, levels * rows), grid_field.dtype)
    )(kernels.T, extended.reshape(levels * rows, -1).T)
    return filtered.T.reshape(levels, rows, lon_width)


def to_columns(grid_field):
    return lax.all_to_all(grid_field, "lat", 2, 1, tiled=True)


def to_rows(grid_field):
    return lax.all_to_all(grid_field, "lat", 1, 2, tiled=True)


def lat_pass(grid_field, matrices, adjoint):
    if adjoint:
        return jnp.sum(matrices[:, :, :, None] * grid_field[:, None, :, :], axis=2)
    return jnp.sum(matrices[:, :, :, None] * grid_field[:, :, None, :], axis=1)


def vertical_mix(matrix, grid_field):
    return jnp.dot(matrix, grid_field.reshape(LEV, -1), precision=HIGHEST).reshape(grid_field.shape)


def total(vals, axes=("lat", "lon")):
    v = jnp.stack(vals)
    for axis in axes:
        n = lax.axis_size(axis)
        g = lax.all_to_all(jnp.broadcast_to(v[None], (n,) + v.shape), axis, 0, 0, tiled=True)
        v = jnp.sum(g, axis=0)
    return tuple(v[i] for i in range(len(vals)))


def update_kernel(scales_ref, iterate_ref, residual_ref, direction_ref, iterate_out, direction_out):
    iterate_out[...] = iterate_ref[...] + scales_ref[0, 0] * direction_ref[...]
    direction_out[...] = residual_ref[...] + scales_ref[0, 1] * direction_ref[...]


def local(iterate, residual, direction, obs_weight, vertical, lon_taps, lat_taps, band_sizes):
    bounds = jnp.cumsum(band_sizes)
    levels = jnp.arange(LEV, dtype=jnp.int32)
    groups = jnp.sum((levels[:, None] >= bounds[None, :]).astype(jnp.int32), axis=1)
    lon_part = lon_pass(direction, lon_taps, groups, False)
    both = to_columns(jnp.concatenate([lon_part, obs_weight], axis=0))
    lat_width = both.shape[1]
    matrices = band_matrices(group_rows(groups, lat_taps), lat_width, lat_width)
    lat_part = lat_pass(both[:LEV], matrices, False)
    lifted = vertical_mix(vertical, lat_part)
    weighted = both[LEV:] * lifted
    partial = jnp.stack(
        [jnp.sum(residual * residual), jnp.sum(direction * direction) + jnp.sum(weighted * lifted)]
    )
    back_vert = vertical_mix(vertical.T, weighted)
    back_cols = lat_pass(back_vert, matrices, True)
    chunk = back_cols.shape[2]
    extra = jnp.zeros((1,) + back_cols.shape[1:], back_cols.dtype).at[0, :, :2].set(partial)
    returned = to_rows(jnp.concatenate([back_cols, extra], axis=0))
    back_lat = returned[:LEV]
    lat_sums = jnp.sum(returned[LEV, 0].reshape(-1, chunk)[:, :2], axis=0)
    norm_old, curvature = total((lat_sums[0], lat_sums[1]), ("lon",))
    applied = lon_pass_add(back_lat, direction, lon_taps, groups)
    step_length = norm_old / curvature
    residual_next = residual - step_length * applied
    (norm_new,) = total((jnp.sum(residual_next * residual_next),))
    scales = jnp.stack([step_length, norm_new / norm_old]).reshape(1, 2)
    iterate_next, direction_next = pl.pallas_call(
        update_kernel,
        out_shape=(
            jax.ShapeDtypeStruct(iterate.shape, iterate.dtype),
            jax.ShapeDtypeStruct(direction.shape, direction.dtype),
        ),
        in_specs=[pl.BlockSpec(memory_space=pltpu.SMEM)] + [pl.BlockSpec()] * 3,
    )(scales, iterate, residual_next, direction)
    return (iterate_next, residual_next, direction_next)


def solution(mesh):
    placed = (
        P(None, "lat", "lon"),
        P(None, "lat", "lon"),
        P(None, "lat", "lon"),
        P(None, "lat", "lon"),
        P(),
        P(),
        P(),
        P(),
    )
    return jax.shard_map(
        local,
        mesh=mesh,
        in_specs=placed,
        out_specs=(P(None, "lat", "lon"), P(None, "lat", "lon"), P(None, "lat", "lon")),
        check_vma=False,
    )
```
